256 devices in a mesh: dp: 2 (over core), ctx: 32 (over y, z), tensor: 4 (over x).
Axes of the slice: x: 4, y: 4, z: 8, core: 2. Of those that a mesh axis runs over, the one named last changes fastest.
Arguments:
- query_in: bfloat16 [2, 8192, 8192], P('dp', 'ctx', 'tensor'), may hold values from -6 to 6
- key_in: bfloat16 [2, 8192, 8192], P('dp', 'ctx', 'tensor'), may hold values from -6 to 6
- value_in: bfloat16 [2, 8192, 8192], P('dp', 'ctx', 'tensor'), may hold values from -6 to 6
- grad_out: bfloat16 [2, 8192, 8192], P('dp', 'ctx', 'tensor'), may hold values from -6 to 6
- seq_lengths: int32 [2, 64], P('dp'), may hold values from 1 to 512, 8192 in all within a row
- filters: bfloat16 [512, 128], P('tensor'), may hold values from -0.5 to 0.5
Outputs:
- mixed_out: bfloat16 [2, 8192, 8192], P('dp', 'ctx', 'tensor')
- grad_query: bfloat16 [2, 8192, 8192], P('dp', 'ctx', 'tensor')
- grad_key: bfloat16 [2, 8192, 8192], P('dp', 'ctx', 'tensor')
- grad_value: bfloat16 [2, 8192, 8192], P('dp', 'ctx', 'tensor')
- grad_filters: float32 [512, 128], P('tensor')
The draws below stay inside these ranges and needn't reach their ends.
All inputs are finite; a program needn't handle non-finite values.
Results may differ from the reference program's by a relative error of at most 0.005.
Values may be sent and summed in bfloat16 or wider, within the bound.
No kernel may reach another device: no remote copies, remote signals or barrier semaphores. Data moves between devices by JAX's collectives and lax.ppermute only.
A program may use at most 192 MiB of HBM per device.

```python
import math
import jax
import jax.numpy as jnp
import numpy as np
from jax import lax

C = 8192
GROUP = 16
FLEN = 128
TOK_DEV = 256
BATCH = 2
LEN = 8192
GROUPS = 512
NSEQ = 64


def steps_of(stream_key, shape, split, smallest, high):
    factor_of = 1.0
    for axis_at, blocks in split:
        draws = jax.random.uniform(jax.random.fold_in(jax.random.fold_in(stream_key, 6), axis_at), (blocks,), jnp.float32, smallest / len(split), high / len(split))
        factor_of = factor_of * jnp.repeat(jnp.exp(draws), shape[axis_at] // blocks).reshape((-1,) + (1,) * (len(shape) - 1 - axis_at))
    return factor_of


def split_up(count, total, bound, slope):
    weights = [(1 << 20) // math.isqrt(standing ** slope) + 1 for standing in range(2, count + 1)]
    rest, counts = total - bound - (count - 1), [1] * (count - 1)
    while rest > 0:
        candidates = [i for i in range(count - 1) if counts[i] < bound]
        mass, remaining = sum([weights[i] for i in candidates]), rest
        for i in candidates:
            more = min(bound - counts[i], max(1, remaining * weights[i] // mass), rest)
            counts[i] = counts[i] + more
            rest = rest - more
    return np.array([bound] + counts)


def uneven(stream_key, count, total, bound, slope):
    if count == 2:
        one = jax.random.randint(stream_key, (), max(1, total - bound), min(bound, total - 1) + 1)
        return jnp.stack([one, total - one])
    sizes = jnp.asarray(split_up(count, total, bound, slope), jnp.int32)
    pairs = (count - 1) // 2
    donor, taker = sizes[1:1 + 2 * pairs:2], sizes[2:2 + 2 * pairs:2]
    slack = jnp.minimum(donor - 1, bound - taker)
    passed = jax.random.randint(jax.random.fold_in(stream_key, 1), (pairs,), 0, 1 << 20) % (slack + 1)
    sizes = sizes.at[1:1 + 2 * pairs:2].set(donor - passed).at[2:2 + 2 * pairs:2].set(taker + passed)
    return sizes[jax.random.permutation(jax.random.fold_in(stream_key, 2), count)]


def noise(own_key, extent, width, bound, cuts=(), kind=jnp.bfloat16):
    factor_of = steps_of(own_key, extent, cuts, -0.22, 0.18) if cuts else 1.0
    drawn = jax.random.normal(own_key, extent, jnp.float32) * width * factor_of
    return jnp.minimum(jnp.maximum(drawn, -bound), bound).astype(kind)


def setup_inputs(seed: int = 0) -> dict:
    key_list = jax.random.split(jax.random.key(seed), 7)
    return {
        "query_in": noise(key_list[0], (BATCH, LEN, C), 1.0, 6.0, ((0, 2), (1, 32), (2, 4))),
        "key_in": noise(key_list[1], (BATCH, LEN, C), 1.0, 6.0, ((0, 2), (1, 32), (2, 4))),
        "value_in": noise(key_list[2], (BATCH, LEN, C), 1.0, 6.0, ((0, 2), (1, 32), (2, 4))),
        "grad_out": noise(key_list[3], (BATCH, LEN, C), 1.0, 6.0, ((0, 2), (1, 32), (2, 4))),
        "seq_lengths": jax.vmap(lambda own: uneven(own, NSEQ, LEN, 2 * TOK_DEV, 2))(jax.random.split(key_list[4], BATCH)).reshape((BATCH, NSEQ)).astype(jnp.int32),
        "filters": noise(key_list[5], (GROUPS, FLEN), FLEN ** -0.5, 0.5, ((0, 4),)),
    }


def reference(query_in, key_in, value_in, grad_out, seq_lengths, filters):
    tap_table = jnp.repeat(filters.astype(jnp.float32), GROUP, axis=0).T
    positions = jnp.arange(LEN, dtype=jnp.int32)
    raw = jnp.zeros((GROUPS, FLEN), jnp.float32)
    outs_mixed, outs_query, outs_key, outs_value = ([], [], [], [])
    for batch_row in range(BATCH):
        lengths = seq_lengths[batch_row]
        starts = jnp.cumsum(lengths) - lengths
        doc_begin = lax.optimization_barrier(jnp.max(jnp.where(starts[None, :] <= positions[:, None], starts[None, :], 0), axis=1)).astype(jnp.int32)
        query = query_in[batch_row].astype(jnp.float32)
        keys = key_in[batch_row].astype(jnp.float32)
        values = value_in[batch_row].astype(jnp.float32)
        gated = (keys * values).astype(jnp.bfloat16)
        cotangent = (grad_out[batch_row].astype(jnp.float32) * query).astype(jnp.bfloat16)
        cot_float = cotangent.astype(jnp.float32)
        u_padded = jnp.concatenate([jnp.zeros((FLEN, C), jnp.bfloat16), gated], axis=0)
        cot_padded = jnp.concatenate([cotangent, jnp.zeros((FLEN, C), jnp.bfloat16)], axis=0)
        begin_padded = jnp.concatenate([doc_begin, jnp.full((FLEN,), LEN, jnp.int32)], axis=0)

        def tap(state_pair, shift_by):
            mixed, grad_gated = state_pair
            window = lax.dynamic_slice_in_dim(u_padded, (FLEN - shift_by).astype(jnp.int32), LEN, 0).astype(jnp.float32)
            causal = (positions - shift_by >= doc_begin).astype(jnp.float32)[:, None]
            tap_gain = lax.dynamic_index_in_dim(tap_table, shift_by, 0, keepdims=True)
            mixed = mixed + causal * tap_gain * window
            cot_window = lax.dynamic_slice_in_dim(cot_padded, shift_by.astype(jnp.int32), LEN, 0).astype(jnp.float32)
            begin_window = lax.dynamic_slice_in_dim(begin_padded, shift_by.astype(jnp.int32), LEN, 0)
            anticausal = (begin_window <= positions).astype(jnp.float32)[:, None]
            grad_gated = grad_gated + anticausal * tap_gain * cot_window
            contrib = lax.optimization_barrier(jnp.sum(causal * cot_float * window, axis=0)).reshape(GROUPS, GROUP).sum(axis=1)
            return ((mixed, grad_gated), contrib)
        start_pair = (jnp.zeros((LEN, C), jnp.float32), jnp.zeros((LEN, C), jnp.float32))
        (mixed, grad_gated), dh_taps = lax.scan(tap, start_pair, jnp.arange(FLEN, dtype=jnp.int32))
        raw = raw + dh_taps.T
        outs_mixed.append((query * mixed).astype(jnp.bfloat16))
        outs_query.append((grad_out[batch_row].astype(jnp.float32) * mixed).astype(jnp.bfloat16))
        outs_key.append((grad_gated * values).astype(jnp.bfloat16))
        outs_value.append((grad_gated * keys).astype(jnp.bfloat16))
    clip_limit = math.sqrt(GROUPS * FLEN)
    grad_norm = jnp.sqrt(jnp.sum(raw * raw))
    factor = jnp.minimum(1.0, clip_limit / grad_norm)
    return (jnp.stack(outs_mixed), jnp.stack(outs_query), jnp.stack(outs_key), jnp.stack(outs_value), raw * factor)
```

```python
import math

import jax
import jax.numpy as jnp
from jax import lax
from jax.sharding import PartitionSpec as P

GROUP = 16
FLEN = 128
GROUPS = 512


def passed_along(value, axis, steps):
    count = lax.axis_size(axis)
    initial, last = (max(0, -steps), min(count, count - steps))
    return lax.ppermute(value, axis, [(source, source + steps) for source in range(initial, last)])


def doubling_sum(value, axis):
    count = lax.axis_size(axis)
    step = 1
    while step < count:
        partner = lax.ppermute(value, axis, [(i, i ^ step) for i in range(count)])
        value = value + partner
        step *= 2
    return value


def on_device(query_in, key_in, value_in, grad_out, seq_lengths, filters):
    query = query_in[0].astype(jnp.float32)
    keys = key_in[0].astype(jnp.float32)
    values = value_in[0].astype(jnp.float32)
    upstream = grad_out[0].astype(jnp.float32)
    lengths = seq_lengths[0]
    starts = jnp.cumsum(lengths) - lengths
    rows_dev, channels = query.shape
    blocks = rows_dev // FLEN
    local_groups = channels // GROUP
    offset = lax.axis_index("ctx") * rows_dev
    gated = (keys * values).astype(jnp.bfloat16)
    cotangent = (upstream * query).astype(jnp.bfloat16)
    gated_cols = gated.reshape(rows_dev, local_groups, GROUP).transpose(1, 2, 0)
    cot_cols = cotangent.reshape(rows_dev, local_groups, GROUP).transpose(1, 2, 0)
    prev_tail = passed_along(gated_cols[:, :, rows_dev - FLEN :], "ctx", 1)
    u_joined = jnp.concatenate([prev_tail, gated_cols], axis=2)
    row_ids = jnp.arange(FLEN, dtype=jnp.int32)[:, None]
    col_ids = jnp.arange(2 * FLEN, dtype=jnp.int32)[None, :]
    lag_table = row_ids - col_ids + FLEN
    inside = (lag_table >= 0) & (lag_table < FLEN)
    reversed_taps = filters[:, ::-1]
    row_pattern = jnp.concatenate(
        [
            jnp.zeros((local_groups, 1), jnp.bfloat16),
            reversed_taps,
            jnp.zeros((local_groups, FLEN), jnp.bfloat16),
        ],
        axis=1,
    )
    tiled = jnp.broadcast_to(row_pattern[:, None, :], (local_groups, FLEN, 2 * FLEN + 1))
    toeplitz = tiled.reshape(local_groups, FLEN * (2 * FLEN + 1))[:, : FLEN * 2 * FLEN].reshape(
        local_groups, FLEN, 2 * FLEN
    )

    def operator_of(block_id):
        tpos = offset + block_id * FLEN + jnp.arange(FLEN, dtype=jnp.int32)
        rpos = offset + (block_id - 1) * FLEN + jnp.arange(2 * FLEN, dtype=jnp.int32)
        doc_begin = jnp.max(jnp.where(starts[None, :] <= tpos[:, None], starts[None, :], 0), axis=1)
        inside_doc = (rpos[None, :] >= doc_begin[:, None]) & inside
        return (toeplitz * inside_doc.astype(jnp.bfloat16)[None], inside_doc.astype(jnp.float32))

    def per_block(accum, block_id):
        operator, valid = operator_of(block_id)
        window = lax.dynamic_slice_in_dim(u_joined, block_id * FLEN, 2 * FLEN, 2)
        cot_block = lax.dynamic_slice_in_dim(cot_cols, block_id * FLEN, FLEN, 2)
        mixed_rows = jnp.einsum(
            "gtr,gcr->gct", operator, window, preferred_element_type=jnp.float32
        )
        back_rows = jnp.einsum(
            "gtr,gct->gcr", operator, cot_block, preferred_element_type=jnp.float32
        )
        products = jnp.einsum("gct,gcr->gtr", cot_block, window, preferred_element_type=jnp.float32)
        accum = accum + products * valid[None]
        return (accum, (mixed_rows, back_rows))

    start_accum = jnp.zeros((local_groups, FLEN, 2 * FLEN), jnp.float32)
    accum, (mixed_blocks, back_blocks) = lax.scan(
        per_block, start_accum, jnp.arange(blocks, dtype=jnp.int32)
    )
    flat = accum.reshape(local_groups, FLEN * 2 * FLEN)
    flat = jnp.pad(flat, ((0, 0), (0, FLEN)))
    skewed = flat.reshape(local_groups, FLEN, 2 * FLEN + 1)
    lag_sums = jnp.sum(skewed, axis=1)[:, 1 : FLEN + 1]
    local_raw = lag_sums[:, ::-1]
    next_head = passed_along(cot_cols[:, :, :FLEN], "ctx", -1)
    next_operator, next_valid = operator_of(blocks)
    spill_last = jnp.einsum(
        "gtr,gct->gcr", next_operator, next_head, preferred_element_type=jnp.float32
    )[:, :, :FLEN]
    own_rows = back_blocks[:, :, :, FLEN:]
    spill_rows = jnp.concatenate([back_blocks[1:, :, :, :FLEN], spill_last[None]], axis=0)
    grad_gated = (own_rows + spill_rows).transpose(0, 3, 1, 2).reshape(rows_dev, channels)
    mixed = mixed_blocks.transpose(0, 3, 1, 2).reshape(rows_dev, channels)
    mixed_out = (query * mixed).astype(jnp.bfloat16)
    grad_query = (upstream * mixed).astype(jnp.bfloat16)
    grad_key = (grad_gated * values).astype(jnp.bfloat16)
    grad_value = (grad_gated * keys).astype(jnp.bfloat16)
    clip_limit = math.sqrt(GROUPS * FLEN)
    summed = doubling_sum(doubling_sum(local_raw, "dp"), "ctx")
    squares = doubling_sum(jnp.sum(summed * summed), "tensor")
    factor = jnp.minimum(1.0, clip_limit / jnp.sqrt(squares))
    grad_filters = summed * factor
    return (mixed_out[None], grad_query[None], grad_key[None], grad_value[None], grad_filters)


def solution(mesh):
    in_specs = (
        P("dp", "ctx", "tensor"),
        P("dp", "ctx", "tensor"),
        P("dp", "ctx", "tensor"),
        P("dp", "ctx", "tensor"),
        P("dp", None),
        P("tensor", None),
    )
    out_specs = (
        P("dp", "ctx", "tensor"),
        P("dp", "ctx", "tensor"),
        P("dp", "ctx", "tensor"),
        P("dp", "ctx", "tensor"),
        P("tensor", None),
    )
    return jax.shard_map(
        on_device, mesh=mesh, in_specs=in_specs, out_specs=out_specs, check_vma=False
    )
```

```python
import math

import jax
import jax.numpy as jnp
from jax import lax
from jax.experimental import pallas as pl
from jax.experimental.pallas import tpu as pltpu
from jax.sharding import PartitionSpec as P

GROUP = 16
FLEN = 128
GROUPS = 512
LANES = 128


def passed_along(value, axis, steps):
    count = lax.axis_size(axis)
    initial, last = (max(0, -steps), min(count, count - steps))
    return lax.ppermute(value, axis, [(source, source + steps) for source in range(initial, last)])


def doubling_sum(value, axis):
    count = lax.axis_size(axis)
    step = 1
    while step < count:
        partner = lax.ppermute(value, axis, [(i, i ^ step) for i in range(count)])
        value = value + partner
        step *= 2
    return value


def conv_kernel(q_ref, k_ref, v_ref, go_ref, prev_ref, next_ref, fp_ref, fq_ref, m_ref, mt_ref, mr_ref,
                mo_ref, gq_ref, gk_ref, gv_ref, raw_ref):
    f32, bf16 = jnp.float32, jnp.bfloat16
    rows = q_ref.shape[0]
    blocks = rows // FLEN
    query = q_ref[...].astype(f32)
    keys = k_ref[...].astype(f32)
    values = v_ref[...].astype(f32)
    upstream = go_ref[...].astype(f32)
    gated = (keys * values).astype(bf16)
    cot = (upstream * query).astype(bf16)
    u_all = jnp.concatenate([prev_ref[...], gated], axis=0)
    c_all = jnp.concatenate([cot, next_ref[...]], axis=0)
    lane_group = lax.broadcasted_iota(jnp.int32, (1, LANES), 1) // GROUP
    windows = [u_all[b * FLEN:(b + 2) * FLEN] for b in range(blocks)]
    cots = [c_all[b * FLEN:(b + 1) * FLEN] for b in range(blocks + 1)]
    masks = [m_ref[b] for b in range(blocks + 1)]
    masks_t = [mt_ref[b] for b in range(blocks + 1)]
    masks_r = [mr_ref[b].astype(f32) for b in range(blocks)]
    flip = (lax.broadcasted_iota(jnp.int32, (FLEN, FLEN), 0)
            + lax.broadcasted_iota(jnp.int32, (FLEN, FLEN), 1) == FLEN - 1).astype(bf16)
    cots_r = [jnp.dot(flip, cots[b], preferred_element_type=f32).astype(bf16) for b in range(blocks)]
    mixed = [jnp.zeros((FLEN, LANES), f32) for _ in range(blocks)]
    back = [jnp.zeros((FLEN, LANES), f32) for _ in range(blocks)]
    nt = (((1,), (1,)), ((), ()))
    sums = []
    for k in range(LANES // GROUP):
        prow = jnp.broadcast_to(fp_ref[k:k + 1, :], (FLEN, 2 * FLEN))
        taps = pltpu.roll(prow, 0, 1, stride=1, stride_axis=0).astype(bf16)
        qrow = jnp.broadcast_to(fq_ref[k:k + 1, :], (2 * FLEN, 2 * FLEN))
        taps_t = pltpu.roll(qrow, FLEN, 1, stride=1, stride_axis=0)[:, :FLEN].astype(bf16)
        in_group = lane_group == k
        group_cots = [jnp.where(in_group, c, jnp.zeros_like(c)) for c in cots]
        group_cots_r = [jnp.where(in_group, c, jnp.zeros_like(c)) for c in cots_r]
        acc = jnp.zeros((FLEN, 2 * FLEN), f32)
        for b in range(blocks):
            window = jnp.where(in_group, windows[b], jnp.zeros_like(windows[b]))
            mixed[b] = mixed[b] + jnp.dot(taps * masks[b], window, preferred_element_type=f32)
            prods = lax.dot_general(group_cots_r[b], windows[b], nt, preferred_element_type=f32)
            acc = acc + prods * masks_r[b]
        for b in range(blocks + 1):
            spread = jnp.dot(taps_t * masks_t[b], group_cots[b], preferred_element_type=f32)
            if b < blocks:
                back[b] = back[b] + spread[FLEN:]
            if b > 0:
                back[b - 1] = back[b - 1] + spread[:FLEN]
        skewed = pltpu.roll(acc, 0, 1, stride=1, stride_axis=0)
        sums.append(jnp.sum(skewed, axis=0, keepdims=True))
    raw_ref[0] = jnp.concatenate(sums, axis=0)
    mixed_all = jnp.concatenate(mixed, axis=0)
    back_all = jnp.concatenate(back, axis=0)
    mo_ref[...] = (query * mixed_all).astype(bf16)
    gq_ref[...] = (upstream * mixed_all).astype(bf16)
    gk_ref[...] = (back_all * values).astype(bf16)
    gv_ref[...] = (back_all * keys).astype(bf16)


def grouped_conv(q2, k2, v2, g2, prev_tail, next_head, fp, fq, mask, mask_t, interpret=False):
    mask_r = mask[:-1, ::-1, :]
    rows, channels = q2.shape
    tiles = channels // LANES
    per_tile = LANES // GROUP
    nb = rows // FLEN
    tok = pl.BlockSpec((rows, LANES), lambda j: (0, j))
    halo = pl.BlockSpec((FLEN, LANES), lambda j: (0, j))
    filt = pl.BlockSpec((per_tile, 2 * FLEN), lambda j: (j, 0))
    mspec = pl.BlockSpec((nb + 1, FLEN, 2 * FLEN), lambda j: (0, 0, 0))
    mtspec = pl.BlockSpec((nb + 1, 2 * FLEN, FLEN), lambda j: (0, 0, 0))
    mrspec = pl.BlockSpec((nb, FLEN, 2 * FLEN), lambda j: (0, 0, 0))
    out_tok = jax.ShapeDtypeStruct((rows, channels), jnp.bfloat16)
    return pl.pallas_call(
        conv_kernel,
        grid=(tiles,),
        in_specs=[tok, tok, tok, tok, halo, halo, filt, filt, mspec, mtspec, mrspec],
        out_specs=[tok, tok, tok, tok, pl.BlockSpec((1, per_tile, 2 * FLEN), lambda j: (j, 0, 0))],
        out_shape=[out_tok, out_tok, out_tok, out_tok,
                   jax.ShapeDtypeStruct((tiles, per_tile, 2 * FLEN), jnp.float32)],
        interpret=interpret,
    )(q2, k2, v2, g2, prev_tail, next_head, fp, fq, mask, mask_t, mask_r)


def doc_masks(lengths, offset, rows):
    starts = jnp.cumsum(lengths) - lengths
    nb = rows // FLEN
    b_ids = jnp.arange(nb + 1, dtype=jnp.int32)[:, None]
    tpos = offset + b_ids * FLEN + jnp.arange(FLEN, dtype=jnp.int32)[None, :]
    doc_begin = jnp.max(jnp.where(starts[None, None, :] <= tpos[:, :, None], starts[None, None, :], 0), axis=2)
    rpos = offset + (b_ids - 1) * FLEN + jnp.arange(2 * FLEN, dtype=jnp.int32)[None, :]
    lag = jnp.arange(FLEN, dtype=jnp.int32)[:, None] + FLEN - jnp.arange(2 * FLEN, dtype=jnp.int32)[None, :]
    inside = (lag >= 0) & (lag < FLEN)
    mask = ((rpos[:, None, :] >= doc_begin[:, :, None]) & inside[None]).astype(jnp.bfloat16)
    return mask, mask.transpose(0, 2, 1)


def filter_rows(filters):
    taps = filters.astype(jnp.float32)
    groups = taps.shape[0]
    fp = jnp.concatenate([jnp.zeros((groups, 1), jnp.float32), taps[:, ::-1],
                          jnp.zeros((groups, FLEN - 1), jnp.float32)], axis=1)
    fq = jnp.concatenate([taps, jnp.zeros((groups, FLEN), jnp.float32)], axis=1)
    return fp, fq


def on_device(query_in, key_in, value_in, grad_out, seq_lengths, filters):
    f32, bf16 = jnp.float32, jnp.bfloat16
    q2, k2, v2, g2 = query_in[0], key_in[0], value_in[0], grad_out[0]
    rows = q2.shape[0]
    tail = (k2[rows - FLEN:].astype(f32) * v2[rows - FLEN:].astype(f32)).astype(bf16)
    head = (g2[:FLEN].astype(f32) * q2[:FLEN].astype(f32)).astype(bf16)
    prev_tail = passed_along(tail, "ctx", 1)
    next_head = passed_along(head, "ctx", -1)
    mask, mask_t = doc_masks(seq_lengths[0], lax.axis_index("ctx") * rows, rows)
    fp, fq = filter_rows(filters)
    mixed_out, grad_query, grad_key, grad_value, cols = grouped_conv(
        q2, k2, v2, g2, prev_tail, next_head, fp, fq, mask, mask_t)
    local_raw = cols.reshape(-1, 2 * FLEN)[:, 2 * FLEN - 1:FLEN - 1:-1]
    summed = doubling_sum(doubling_sum(local_raw, "dp"), "ctx")
    squares = doubling_sum(jnp.sum(summed * summed), "tensor")
    factor = jnp.minimum(1.0, math.sqrt(GROUPS * FLEN) / jnp.sqrt(squares))
    grad_filters = summed * factor
    return (mixed_out[None], grad_query[None], grad_key[None], grad_value[None], grad_filters)


def solution(mesh):
    tok = P("dp", "ctx", "tensor")
    in_specs = (tok, tok, tok, tok, P("dp", None), P("tensor", None))
    out_specs = (tok, tok, tok, tok, P("tensor", None))
    return jax.shard_map(
        on_device, mesh=mesh, in_specs=in_specs, out_specs=out_specs, check_vma=False
    )
```

```python
import math

import jax
import jax.numpy as jnp
from jax import lax
from jax.experimental import pallas as pl
from jax.experimental.pallas import tpu as pltpu
from jax.sharding import PartitionSpec as P

GROUP = 16
FLEN = 128
GROUPS = 512
LANES = 128


def passed_along(value, axis, steps):
    count = lax.axis_size(axis)
    initial, last = (max(0, -steps), min(count, count - steps))
    return lax.ppermute(value, axis, [(source, source + steps) for source in range(initial, last)])


def doubling_sum(value, axis):
    count = lax.axis_size(axis)
    step = 1
    while step < count:
        partner = lax.ppermute(value, axis, [(i, i ^ step) for i in range(count)])
        value = value + partner
        step *= 2
    return value


def radix_sum(value, axes, bits):
    sizes = [lax.axis_size(a) for a in axes]
    count = math.prod(sizes)
    linear = 0
    for a, n in zip(axes, sizes):
        linear = linear * n + lax.axis_index(a)
    members = [m for m in range(count) if m & bits == m]
    received = [value] + [
        lax.ppermute(value, axes, [(i, i ^ m) for i in range(count)]) for m in members[1:]
    ]
    table = jnp.array(members, jnp.int32)
    picks = jnp.searchsorted(table, (linear & bits) ^ table)
    return jnp.sum(jnp.take(jnp.stack(received), picks, axis=0), axis=0)


def conv_kernel(q_ref, k_ref, v_ref, go_ref, prev_ref, next_ref, fp_ref, fq_ref, m_ref, mt_ref, mr_ref,
                mo_ref, gq_ref, gk_ref, gv_ref, raw_ref):
    f32, bf16 = jnp.float32, jnp.bfloat16
    rows = q_ref.shape[0]
    blocks = rows // FLEN
    query = q_ref[...].astype(f32)
    keys = k_ref[...].astype(f32)
    values = v_ref[...].astype(f32)
    upstream = go_ref[...].astype(f32)
    gated = (keys * values).astype(bf16)
    cot = (upstream * query).astype(bf16)
    u_all = jnp.concatenate([prev_ref[...], gated], axis=0)
    c_all = jnp.concatenate([cot, next_ref[...]], axis=0)
    lane_group = lax.broadcasted_iota(jnp.int32, (1, LANES), 1) // GROUP
    windows = [u_all[b * FLEN:(b + 2) * FLEN] for b in range(blocks)]
    cots = [c_all[b * FLEN:(b + 1) * FLEN] for b in range(blocks + 1)]
    masks = [m_ref[b] for b in range(blocks + 1)]
    masks_t = [mt_ref[b] for b in range(blocks + 1)]
    masks_r = [mr_ref[b].astype(f32) for b in range(blocks)]
    flip = (lax.broadcasted_iota(jnp.int32, (FLEN, FLEN), 0)
            + lax.broadcasted_iota(jnp.int32, (FLEN, FLEN), 1) == FLEN - 1).astype(bf16)
    cots_r = [jnp.dot(flip, cots[b], preferred_element_type=f32).astype(bf16) for b in range(blocks)]
    mixed = [jnp.zeros((FLEN, LANES), f32) for _ in range(blocks)]
    back = [jnp.zeros((FLEN, LANES), f32) for _ in range(blocks)]
    nt = (((1,), (1,)), ((), ()))
    sums = []
    for k in range(LANES // GROUP):
        prow = jnp.broadcast_to(fp_ref[k:k + 1, :], (FLEN, 2 * FLEN))
        taps = pltpu.roll(prow, 0, 1, stride=1, stride_axis=0).astype(bf16)
        qrow = jnp.broadcast_to(fq_ref[k:k + 1, :], (2 * FLEN, 2 * FLEN))
        taps_t = pltpu.roll(qrow, FLEN, 1, stride=1, stride_axis=0)[:, :FLEN].astype(bf16)
        in_group = lane_group == k
        group_cots = [jnp.where(in_group, c, jnp.zeros_like(c)) for c in cots]
        group_cots_r = [jnp.where(in_group, c, jnp.zeros_like(c)) for c in cots_r]
        acc = jnp.zeros((FLEN, 2 * FLEN), f32)
        for b in range(blocks):
            window = jnp.where(in_group, windows[b], jnp.zeros_like(windows[b]))
            mixed[b] = mixed[b] + jnp.dot(taps * masks[b], window, preferred_element_type=f32)
            prods = lax.dot_general(group_cots_r[b], windows[b], nt, preferred_element_type=f32)
            acc = acc + prods * masks_r[b]
        for b in range(blocks + 1):
            spread = jnp.dot(taps_t * masks_t[b], group_cots[b], preferred_element_type=f32)
            if b < blocks:
                back[b] = back[b] + spread[FLEN:]
            if b > 0:
                back[b - 1] = back[b - 1] + spread[:FLEN]
        skewed = pltpu.roll(acc, 0, 1, stride=1, stride_axis=0)
        sums.append(jnp.sum(skewed, axis=0, keepdims=True))
    raw_ref[0] = jnp.concatenate(sums, axis=0)
    mixed_all = jnp.concatenate(mixed, axis=0)
    back_all = jnp.concatenate(back, axis=0)
    mo_ref[...] = (query * mixed_all).astype(bf16)
    gq_ref[...] = (upstream * mixed_all).astype(bf16)
    gk_ref[...] = (back_all * values).astype(bf16)
    gv_ref[...] = (back_all * keys).astype(bf16)


def grouped_conv(q2, k2, v2, g2, prev_tail, next_head, fp, fq, mask, mask_t, interpret=False):
    mask_r = mask[:-1, ::-1, :]
    rows, channels = q2.shape
    tiles = channels // LANES
    per_tile = LANES // GROUP
    nb = rows // FLEN
    tok = pl.BlockSpec((rows, LANES), lambda j: (0, j))
    halo = pl.BlockSpec((FLEN, LANES), lambda j: (0, j))
    filt = pl.BlockSpec((per_tile, 2 * FLEN), lambda j: (j, 0))
    mspec = pl.BlockSpec((nb + 1, FLEN, 2 * FLEN), lambda j: (0, 0, 0))
    mtspec = pl.BlockSpec((nb + 1, 2 * FLEN, FLEN), lambda j: (0, 0, 0))
    mrspec = pl.BlockSpec((nb, FLEN, 2 * FLEN), lambda j: (0, 0, 0))
    out_tok = jax.ShapeDtypeStruct((rows, channels), jnp.bfloat16)
    return pl.pallas_call(
        conv_kernel,
        grid=(tiles,),
        in_specs=[tok, tok, tok, tok, halo, halo, filt, filt, mspec, mtspec, mrspec],
        out_specs=[tok, tok, tok, tok, pl.BlockSpec((1, per_tile, 2 * FLEN), lambda j: (j, 0, 0))],
        out_shape=[out_tok, out_tok, out_tok, out_tok,
                   jax.ShapeDtypeStruct((tiles, per_tile, 2 * FLEN), jnp.float32)],
        interpret=interpret,
    )(q2, k2, v2, g2, prev_tail, next_head, fp, fq, mask, mask_t, mask_r)


def doc_masks(lengths, offset, rows):
    starts = jnp.cumsum(lengths) - lengths
    nb = rows // FLEN
    b_ids = jnp.arange(nb + 1, dtype=jnp.int32)[:, None]
    tpos = offset + b_ids * FLEN + jnp.arange(FLEN, dtype=jnp.int32)[None, :]
    doc_begin = jnp.max(jnp.where(starts[None, None, :] <= tpos[:, :, None], starts[None, None, :], 0), axis=2)
    rpos = offset + (b_ids - 1) * FLEN + jnp.arange(2 * FLEN, dtype=jnp.int32)[None, :]
    lag = jnp.arange(FLEN, dtype=jnp.int32)[:, None] + FLEN - jnp.arange(2 * FLEN, dtype=jnp.int32)[None, :]
    inside = (lag >= 0) & (lag < FLEN)
    mask = ((rpos[:, None, :] >= doc_begin[:, :, None]) & inside[None]).astype(jnp.bfloat16)
    return mask, mask.transpose(0, 2, 1)


def filter_rows(filters):
    taps = filters.astype(jnp.float32)
    groups = taps.shape[0]
    fp = jnp.concatenate([jnp.zeros((groups, 1), jnp.float32), taps[:, ::-1],
                          jnp.zeros((groups, FLEN - 1), jnp.float32)], axis=1)
    fq = jnp.concatenate([taps, jnp.zeros((groups, FLEN), jnp.float32)], axis=1)
    return fp, fq


def on_device(query_in, key_in, value_in, grad_out, seq_lengths, filters):
    f32, bf16 = jnp.float32, jnp.bfloat16
    q2, k2, v2, g2 = query_in[0], key_in[0], value_in[0], grad_out[0]
    rows = q2.shape[0]
    tail = (k2[rows - FLEN:].astype(f32) * v2[rows - FLEN:].astype(f32)).astype(bf16)
    head = (g2[:FLEN].astype(f32) * q2[:FLEN].astype(f32)).astype(bf16)
    prev_tail = passed_along(tail, "ctx", 1)
    next_head = passed_along(head, "ctx", -1)
    mask, mask_t = doc_masks(seq_lengths[0], lax.axis_index("ctx") * rows, rows)
    fp, fq = filter_rows(filters)
    mixed_out, grad_query, grad_key, grad_value, cols = grouped_conv(
        q2, k2, v2, g2, prev_tail, next_head, fp, fq, mask, mask_t)
    local_raw = cols.reshape(-1, 2 * FLEN)[:, 2 * FLEN - 1:FLEN - 1:-1]
    near = radix_sum(local_raw, ("ctx",), 7)
    summed = radix_sum(near, ("dp", "ctx"), 56)
    squares = radix_sum(jnp.sum(summed * summed), ("tensor",), 3)
    factor = jnp.minimum(1.0, math.sqrt(GROUPS * FLEN) / jnp.sqrt(squares))
    grad_filters = summed * factor
    return (mixed_out[None], grad_query[None], grad_key[None], grad_value[None], grad_filters)


def solution(mesh):
    tok = P("dp", "ctx", "tensor")
    in_specs = (tok, tok, tok, tok, P("dp", None), P("tensor", None))
    out_specs = (tok, tok, tok, tok, P("tensor", None))
    return jax.shard_map(
        on_device, mesh=mesh, in_specs=in_specs, out_specs=out_specs, check_vma=False
    )
```

```python
import math

import jax
import jax.numpy as jnp
from jax import lax
from jax.experimental import pallas as pl
from jax.experimental.pallas import tpu as pltpu
from jax.sharding import PartitionSpec as P

GROUP = 16
FLEN = 128
GROUPS = 512
LANES = 128


def passed_along(value, axis, steps):
    count = lax.axis_size(axis)
    initial, last = (max(0, -steps), min(count, count - steps))
    return lax.ppermute(value, axis, [(source, source + steps) for source in range(initial, last)])


def doubling_sum(value, axis):
    count = lax.axis_size(axis)
    step = 1
    while step < count:
        partner = lax.ppermute(value, axis, [(i, i ^ step) for i in range(count)])
        value = value + partner
        step *= 2
    return value


def raw_kernel(q_ref, k_ref, v_ref, go_ref, prev_ref, mr_ref, raw_ref):
    f32, bf16 = jnp.float32, jnp.bfloat16
    rows = q_ref.shape[0]
    blocks = rows // FLEN
    gated = (k_ref[...].astype(f32) * v_ref[...].astype(f32)).astype(bf16)
    cot = (go_ref[...].astype(f32) * q_ref[...].astype(f32)).astype(bf16)
    u_all = jnp.concatenate([prev_ref[...], gated], axis=0)
    lane_group = lax.broadcasted_iota(jnp.int32, (1, LANES), 1) // GROUP
    windows = [u_all[b * FLEN:(b + 2) * FLEN] for b in range(blocks)]
    masks_r = [mr_ref[b].astype(f32) for b in range(blocks)]
    flip = (lax.broadcasted_iota(jnp.int32, (FLEN, FLEN), 0)
            + lax.broadcasted_iota(jnp.int32, (FLEN, FLEN), 1) == FLEN - 1).astype(bf16)
    cots_r = [jnp.dot(flip, cot[b * FLEN:(b + 1) * FLEN], preferred_element_type=f32).astype(bf16)
              for b in range(blocks)]
    nt = (((1,), (1,)), ((), ()))
    sums = []
    for k in range(LANES // GROUP):
        in_group = lane_group == k
        acc = jnp.zeros((FLEN, 2 * FLEN), f32)
        for b in range(blocks):
            group_cot = jnp.where(in_group, cots_r[b], jnp.zeros_like(cots_r[b]))
            prods = lax.dot_general(group_cot, windows[b], nt, preferred_element_type=f32)
            acc = acc + prods * masks_r[b]
        skewed = pltpu.roll(acc, 0, 1, stride=1, stride_axis=0)
        sums.append(jnp.sum(skewed, axis=0, keepdims=True))
    raw_ref[0] = jnp.concatenate(sums, axis=0)


def conv_kernel(q_ref, k_ref, v_ref, go_ref, prev_ref, next_ref, fp_ref, fq_ref, m_ref, mt_ref, *refs):
    mo_ref, gq_ref, gk_ref, gv_ref = refs[-4:]
    f32, bf16 = jnp.float32, jnp.bfloat16
    rows = q_ref.shape[0]
    blocks = rows // FLEN
    query = q_ref[...].astype(f32)
    keys = k_ref[...].astype(f32)
    values = v_ref[...].astype(f32)
    upstream = go_ref[...].astype(f32)
    gated = (keys * values).astype(bf16)
    cot = (upstream * query).astype(bf16)
    u_all = jnp.concatenate([prev_ref[...], gated], axis=0)
    c_all = jnp.concatenate([cot, next_ref[...]], axis=0)
    lane_group = lax.broadcasted_iota(jnp.int32, (1, LANES), 1) // GROUP
    windows = [u_all[b * FLEN:(b + 2) * FLEN] for b in range(blocks)]
    cots = [c_all[b * FLEN:(b + 1) * FLEN] for b in range(blocks + 1)]
    masks = [m_ref[b] for b in range(blocks + 1)]
    masks_t = [mt_ref[b] for b in range(blocks + 1)]
    mixed = [jnp.zeros((FLEN, LANES), f32) for _ in range(blocks)]
    back = [jnp.zeros((FLEN, LANES), f32) for _ in range(blocks)]
    for k in range(LANES // GROUP):
        prow = jnp.broadcast_to(fp_ref[k:k + 1, :], (FLEN, 2 * FLEN))
        taps = pltpu.roll(prow, 0, 1, stride=1, stride_axis=0).astype(bf16)
        qrow = jnp.broadcast_to(fq_ref[k:k + 1, :], (2 * FLEN, 2 * FLEN))
        taps_t = pltpu.roll(qrow, FLEN, 1, stride=1, stride_axis=0)[:, :FLEN].astype(bf16)
        in_group = lane_group == k
        group_cots = [jnp.where(in_group, c, jnp.zeros_like(c)) for c in cots]
        for b in range(blocks):
            window = jnp.where(in_group, windows[b], jnp.zeros_like(windows[b]))
            mixed[b] = mixed[b] + jnp.dot(taps * masks[b], window, preferred_element_type=f32)
        for b in range(blocks + 1):
            spread = jnp.dot(taps_t * masks_t[b], group_cots[b], preferred_element_type=f32)
            if b < blocks:
                back[b] = back[b] + spread[FLEN:]
            if b > 0:
                back[b - 1] = back[b - 1] + spread[:FLEN]
    mixed_all = jnp.concatenate(mixed, axis=0)
    back_all = jnp.concatenate(back, axis=0)
    mo_ref[...] = (query * mixed_all).astype(bf16)
    gq_ref[...] = (upstream * mixed_all).astype(bf16)
    gk_ref[...] = (back_all * values).astype(bf16)
    gv_ref[...] = (back_all * keys).astype(bf16)


def raw_terms(q2, k2, v2, g2, prev_tail, mask, interpret=False):
    rows, channels = q2.shape
    tiles = channels // LANES
    per_tile = LANES // GROUP
    nb = rows // FLEN
    mask_r = mask[:-1, ::-1, :]
    tok = pl.BlockSpec((rows, LANES), lambda j: (0, j))
    halo = pl.BlockSpec((FLEN, LANES), lambda j: (0, j))
    mrspec = pl.BlockSpec((nb, FLEN, 2 * FLEN), lambda j: (0, 0, 0))
    return pl.pallas_call(
        raw_kernel,
        grid=(tiles,),
        in_specs=[tok, tok, tok, tok, halo, mrspec],
        out_specs=pl.BlockSpec((1, per_tile, 2 * FLEN), lambda j: (j, 0, 0)),
        out_shape=jax.ShapeDtypeStruct((tiles, per_tile, 2 * FLEN), jnp.float32),
        interpret=interpret,
    )(q2, k2, v2, g2, prev_tail, mask_r)


def conv_part(args, first, count, outs=None, interpret=False):
    q2 = args[0]
    rows, channels = q2.shape
    per_tile = LANES // GROUP
    nb = rows // FLEN
    tok = pl.BlockSpec((rows, LANES), lambda j: (0, j + first))
    halo = pl.BlockSpec((FLEN, LANES), lambda j: (0, j + first))
    filt = pl.BlockSpec((per_tile, 2 * FLEN), lambda j: (j + first, 0))
    mspec = pl.BlockSpec((nb + 1, FLEN, 2 * FLEN), lambda j: (0, 0, 0))
    mtspec = pl.BlockSpec((nb + 1, 2 * FLEN, FLEN), lambda j: (0, 0, 0))
    in_specs = [tok, tok, tok, tok, halo, halo, filt, filt, mspec, mtspec]
    operands = list(args)
    aliases = {}
    if outs is not None:
        for i, o in enumerate(outs):
            aliases[len(operands)] = i
            operands.append(o)
            in_specs.append(pl.BlockSpec(memory_space=pl.ANY))
    out_tok = jax.ShapeDtypeStruct((rows, channels), jnp.bfloat16)
    return pl.pallas_call(
        conv_kernel,
        grid=(count,),
        in_specs=in_specs,
        out_specs=[tok, tok, tok, tok],
        out_shape=[out_tok] * 4,
        input_output_aliases=aliases,
        interpret=interpret,
    )(*operands)


def grouped_conv(q2, k2, v2, g2, prev_tail, next_head, fp, fq, mask, mask_t, parts=4, interpret=False):
    tiles = q2.shape[1] // LANES
    args = (q2, k2, v2, g2, prev_tail, next_head, fp, fq, mask, mask_t)
    cols = raw_terms(q2, k2, v2, g2, prev_tail, mask, interpret=interpret)
    outs = None
    step = tiles // parts
    for p in range(parts):
        outs = conv_part(args, p * step, step, outs, interpret=interpret)
    return (*outs, cols)


def doc_masks(lengths, offset, rows):
    starts = jnp.cumsum(lengths) - lengths
    nb = rows // FLEN
    b_ids = jnp.arange(nb + 1, dtype=jnp.int32)[:, None]
    tpos = offset + b_ids * FLEN + jnp.arange(FLEN, dtype=jnp.int32)[None, :]
    doc_begin = jnp.max(jnp.where(starts[None, None, :] <= tpos[:, :, None], starts[None, None, :], 0), axis=2)
    rpos = offset + (b_ids - 1) * FLEN + jnp.arange(2 * FLEN, dtype=jnp.int32)[None, :]
    lag = jnp.arange(FLEN, dtype=jnp.int32)[:, None] + FLEN - jnp.arange(2 * FLEN, dtype=jnp.int32)[None, :]
    inside = (lag >= 0) & (lag < FLEN)
    mask = ((rpos[:, None, :] >= doc_begin[:, :, None]) & inside[None]).astype(jnp.bfloat16)
    return mask, mask.transpose(0, 2, 1)


def filter_rows(filters):
    taps = filters.astype(jnp.float32)
    groups = taps.shape[0]
    fp = jnp.concatenate([jnp.zeros((groups, 1), jnp.float32), taps[:, ::-1],
                          jnp.zeros((groups, FLEN - 1), jnp.float32)], axis=1)
    fq = jnp.concatenate([taps, jnp.zeros((groups, FLEN), jnp.float32)], axis=1)
    return fp, fq


def exchange_round(value, axis, step):
    count = lax.axis_size(axis)
    partner = lax.ppermute(value, axis, [(i, i ^ step) for i in range(count)])
    return value + partner


def on_device(query_in, key_in, value_in, grad_out, seq_lengths, filters):
    f32, bf16 = jnp.float32, jnp.bfloat16
    q2, k2, v2, g2 = query_in[0], key_in[0], value_in[0], grad_out[0]
    rows, channels = q2.shape
    tail = (k2[rows - FLEN:].astype(f32) * v2[rows - FLEN:].astype(f32)).astype(bf16)
    head = (g2[:FLEN].astype(f32) * q2[:FLEN].astype(f32)).astype(bf16)
    prev_tail = passed_along(tail, "ctx", 1)
    next_head = passed_along(head, "ctx", -1)
    mask, mask_t = doc_masks(seq_lengths[0], lax.axis_index("ctx") * rows, rows)
    fp, fq = filter_rows(filters)
    cols = raw_terms(q2, k2, v2, g2, prev_tail, mask)
    local_raw = cols.reshape(-1, 2 * FLEN)[:, 2 * FLEN - 1:FLEN - 1:-1]
    rounds = [("dp", 1 << i) for i in range(lax.axis_size("dp").bit_length() - 1)]
    rounds += [("ctx", 1 << i) for i in range(lax.axis_size("ctx").bit_length() - 1)]
    tensor_rounds = [("tensor", 1 << i) for i in range(lax.axis_size("tensor").bit_length() - 1)]
    stages = len(rounds) + len(tensor_rounds)
    tiles = channels // LANES
    parts = stages if tiles % stages == 0 else 1
    step = tiles // parts
    args = (q2, k2, v2, g2, prev_tail, next_head, fp, fq, mask, mask_t)
    outs = None
    summed = local_raw
    squares = None
    for stage in range(stages):
        if stage < len(rounds):
            summed = exchange_round(summed, *rounds[stage])
            if stage == len(rounds) - 1:
                squares = jnp.sum(summed * summed)
        else:
            squares = exchange_round(squares, *tensor_rounds[stage - len(rounds)])
        if stage < parts:
            outs = conv_part(args, stage * step, step, outs)
        if squares is None:
            summed, outs = lax.optimization_barrier((summed, outs))
        else:
            summed, squares, outs = lax.optimization_barrier((summed, squares, outs))
    mixed_out, grad_query, grad_key, grad_value = outs
    factor = jnp.minimum(1.0, math.sqrt(GROUPS * FLEN) / jnp.sqrt(squares))
    grad_filters = summed * factor
    return (mixed_out[None], grad_query[None], grad_key[None], grad_value[None], grad_filters)


def solution(mesh):
    tok = P("dp", "ctx", "tensor")
    in_specs = (tok, tok, tok, tok, P("dp", None), P("tensor", None))
    out_specs = (tok, tok, tok, tok, P("tensor", None))
    return jax.shard_map(
        on_device, mesh=mesh, in_specs=in_specs, out_specs=out_specs, check_vma=False
    )
```

```python
import math

import jax
import jax.numpy as jnp
from jax import lax
from jax.experimental import pallas as pl
from jax.experimental.pallas import tpu as pltpu
from jax.sharding import PartitionSpec as P

GROUP = 16
FLEN = 128
GROUPS = 512
LANES = 128


def passed_along(value, axis, steps):
    count = lax.axis_size(axis)
    initial, last = (max(0, -steps), min(count, count - steps))
    return lax.ppermute(value, axis, [(source, source + steps) for source in range(initial, last)])


def doubling_sum(value, axis):
    count = lax.axis_size(axis)
    step = 1
    while step < count:
        partner = lax.ppermute(value, axis, [(i, i ^ step) for i in range(count)])
        value = value + partner
        step *= 2
    return value


def conv_kernel(q_ref, k_ref, v_ref, go_ref, prev_ref, next_ref, fp_ref, fq_ref, m_ref, mt_ref, mr_ref,
                mo_ref, gq_ref, gk_ref, gv_ref, raw_ref):
    f32, bf16 = jnp.float32, jnp.bfloat16
    rows = q_ref.shape[0]
    blocks = rows // FLEN
    query = q_ref[...].astype(f32)
    keys = k_ref[...].astype(f32)
    values = v_ref[...].astype(f32)
    upstream = go_ref[...].astype(f32)
    gated = (keys * values).astype(bf16)
    cot = (upstream * query).astype(bf16)
    u_all = jnp.concatenate([prev_ref[...], gated], axis=0)
    c_all = jnp.concatenate([cot, next_ref[...]], axis=0)
    lane_group = lax.broadcasted_iota(jnp.int32, (1, LANES), 1) // GROUP
    windows = [u_all[b * FLEN:(b + 2) * FLEN] for b in range(blocks)]
    cots = [c_all[b * FLEN:(b + 1) * FLEN] for b in range(blocks + 1)]
    masks = [m_ref[b] for b in range(blocks + 1)]
    masks_t = [mt_ref[b] for b in range(blocks + 1)]
    masks_r = [mr_ref[b].astype(f32) for b in range(blocks)]
    flip = (lax.broadcasted_iota(jnp.int32, (FLEN, FLEN), 0)
            + lax.broadcasted_iota(jnp.int32, (FLEN, FLEN), 1) == FLEN - 1).astype(bf16)
    cots_r = [jnp.dot(flip, cots[b], preferred_element_type=f32).astype(bf16) for b in range(blocks)]
    mixed = [jnp.zeros((FLEN, LANES), f32) for _ in range(blocks)]
    back = [jnp.zeros((FLEN, LANES), f32) for _ in range(blocks)]
    per_tile = LANES // GROUP
    windows_t = [w.astype(f32).T.astype(bf16) for w in windows]
    acc = jnp.zeros((per_tile, FLEN, 2 * FLEN), f32)
    for b in range(blocks):
        stacked = jnp.concatenate(
            [jnp.where(lane_group == k, cots_r[b], jnp.zeros_like(cots_r[b])) for k in range(per_tile)], axis=0)
        prods = jnp.dot(stacked, windows_t[b], preferred_element_type=f32)
        acc = acc + prods.reshape(per_tile, FLEN, 2 * FLEN) * masks_r[b][None]
    skewed = pltpu.roll(acc.reshape(per_tile * FLEN, 2 * FLEN), 0, 1, stride=1, stride_axis=0)
    raw_ref[0] = jnp.sum(skewed.reshape(per_tile, FLEN, 2 * FLEN), axis=1)
    for k in range(per_tile):
        prow = jnp.broadcast_to(fp_ref[k:k + 1, :], (FLEN, 2 * FLEN))
        taps = pltpu.roll(prow, 0, 1, stride=1, stride_axis=0).astype(bf16)
        qrow = jnp.broadcast_to(fq_ref[k:k + 1, :], (2 * FLEN, 2 * FLEN))
        taps_t = pltpu.roll(qrow, FLEN, 1, stride=1, stride_axis=0)[:, :FLEN].astype(bf16)
        in_group = lane_group == k
        group_cots = [jnp.where(in_group, c, jnp.zeros_like(c)) for c in cots]
        for b in range(blocks):
            window = jnp.where(in_group, windows[b], jnp.zeros_like(windows[b]))
            mixed[b] = mixed[b] + jnp.dot(taps * masks[b], window, preferred_element_type=f32)
        for b in range(blocks + 1):
            spread = jnp.dot(taps_t * masks_t[b], group_cots[b], preferred_element_type=f32)
            if b < blocks:
                back[b] = back[b] + spread[FLEN:]
            if b > 0:
                back[b - 1] = back[b - 1] + spread[:FLEN]
    mixed_all = jnp.concatenate(mixed, axis=0)
    back_all = jnp.concatenate(back, axis=0)
    mo_ref[...] = (query * mixed_all).astype(bf16)
    gq_ref[...] = (upstream * mixed_all).astype(bf16)
    gk_ref[...] = (back_all * values).astype(bf16)
    gv_ref[...] = (back_all * keys).astype(bf16)


def grouped_conv(q2, k2, v2, g2, prev_tail, next_head, fp, fq, mask, mask_t, interpret=False):
    mask_r = mask[:-1, ::-1, :]
    rows, channels = q2.shape
    tiles = channels // LANES
    per_tile = LANES // GROUP
    nb = rows // FLEN
    tok = pl.BlockSpec((rows, LANES), lambda j: (0, j))
    halo = pl.BlockSpec((FLEN, LANES), lambda j: (0, j))
    filt = pl.BlockSpec((per_tile, 2 * FLEN), lambda j: (j, 0))
    mspec = pl.BlockSpec((nb + 1, FLEN, 2 * FLEN), lambda j: (0, 0, 0))
    mtspec = pl.BlockSpec((nb + 1, 2 * FLEN, FLEN), lambda j: (0, 0, 0))
    mrspec = pl.BlockSpec((nb, FLEN, 2 * FLEN), lambda j: (0, 0, 0))
    out_tok = jax.ShapeDtypeStruct((rows, channels), jnp.bfloat16)
    return pl.pallas_call(
        conv_kernel,
        grid=(tiles,),
        in_specs=[tok, tok, tok, tok, halo, halo, filt, filt, mspec, mtspec, mrspec],
        out_specs=[tok, tok, tok, tok, pl.BlockSpec((1, per_tile, 2 * FLEN), lambda j: (j, 0, 0))],
        out_shape=[out_tok, out_tok, out_tok, out_tok,
                   jax.ShapeDtypeStruct((tiles, per_tile, 2 * FLEN), jnp.float32)],
        interpret=interpret,
    )(q2, k2, v2, g2, prev_tail, next_head, fp, fq, mask, mask_t, mask_r)


def doc_masks(lengths, offset, rows):
    starts = jnp.cumsum(lengths) - lengths
    nb = rows // FLEN
    b_ids = jnp.arange(nb + 1, dtype=jnp.int32)[:, None]
    tpos = offset + b_ids * FLEN + jnp.arange(FLEN, dtype=jnp.int32)[None, :]
    doc_begin = jnp.max(jnp.where(starts[None, None, :] <= tpos[:, :, None], starts[None, None, :], 0), axis=2)
    rpos = offset + (b_ids - 1) * FLEN + jnp.arange(2 * FLEN, dtype=jnp.int32)[None, :]
    lag = jnp.arange(FLEN, dtype=jnp.int32)[:, None] + FLEN - jnp.arange(2 * FLEN, dtype=jnp.int32)[None, :]
    inside = (lag >= 0) & (lag < FLEN)
    mask = ((rpos[:, None, :] >= doc_begin[:, :, None]) & inside[None]).astype(jnp.bfloat16)
    return mask, mask.transpose(0, 2, 1)


def filter_rows(filters):
    taps = filters.astype(jnp.float32)
    groups = taps.shape[0]
    fp = jnp.concatenate([jnp.zeros((groups, 1), jnp.float32), taps[:, ::-1],
                          jnp.zeros((groups, FLEN - 1), jnp.float32)], axis=1)
    fq = jnp.concatenate([taps, jnp.zeros((groups, FLEN), jnp.float32)], axis=1)
    return fp, fq


def on_device(query_in, key_in, value_in, grad_out, seq_lengths, filters):
    f32, bf16 = jnp.float32, jnp.bfloat16
    q2, k2, v2, g2 = query_in[0], key_in[0], value_in[0], grad_out[0]
    rows = q2.shape[0]
    tail = (k2[rows - FLEN:].astype(f32) * v2[rows - FLEN:].astype(f32)).astype(bf16)
    head = (g2[:FLEN].astype(f32) * q2[:FLEN].astype(f32)).astype(bf16)
    prev_tail = passed_along(tail, "ctx", 1)
    next_head = passed_along(head, "ctx", -1)
    mask, mask_t = doc_masks(seq_lengths[0], lax.axis_index("ctx") * rows, rows)
    fp, fq = filter_rows(filters)
    mixed_out, grad_query, grad_key, grad_value, cols = grouped_conv(
        q2, k2, v2, g2, prev_tail, next_head, fp, fq, mask, mask_t)
    half_turn = jnp.arange(cols.shape[1]) % 2 == 1
    cols = jnp.where(half_turn[None, :, None], jnp.roll(cols, FLEN, axis=2), cols)
    local_raw = cols.reshape(-1, 2 * FLEN)[:, 2 * FLEN - 1:FLEN - 1:-1]
    summed = doubling_sum(doubling_sum(local_raw, "dp"), "ctx")
    squares = doubling_sum(jnp.sum(summed * summed), "tensor")
    factor = jnp.minimum(1.0, math.sqrt(GROUPS * FLEN) / jnp.sqrt(squares))
    grad_filters = summed * factor
    return (mixed_out[None], grad_query[None], grad_key[None], grad_value[None], grad_filters)


def solution(mesh):
    tok = P("dp", "ctx", "tensor")
    in_specs = (tok, tok, tok, tok, P("dp", None), P("tensor", None))
    out_specs = (tok, tok, tok, tok, P("tensor", None))
    return jax.shard_map(
        on_device, mesh=mesh, in_specs=in_specs, out_specs=out_specs, check_vma=False
    )
```

```python
import math

import jax
import jax.numpy as jnp
from jax import lax
from jax.experimental import pallas as pl
from jax.experimental.pallas import tpu as pltpu
from jax.sharding import PartitionSpec as P

GROUP = 16
FLEN = 128
GROUPS = 512
LANES = 128


def passed_along(value, axis, steps):
    count = lax.axis_size(axis)
    initial, last = (max(0, -steps), min(count, count - steps))
    return lax.ppermute(value, axis, [(source, source + steps) for source in range(initial, last)])


def doubling_sum(value, axis):
    count = lax.axis_size(axis)
    step = 1
    while step < count:
        partner = lax.ppermute(value, axis, [(i, i ^ step) for i in range(count)])
        value = value + partner
        step *= 2
    return value


def conv_kernel(q_ref, k_ref, v_ref, go_ref, prev_ref, next_ref, fp_ref, fq_ref, m_ref, mt_ref, mr_ref,
                mo_ref, gq_ref, gk_ref, gv_ref, raw_ref):
    f32, bf16 = jnp.float32, jnp.bfloat16
    rows = q_ref.shape[0]
    blocks = rows // FLEN
    query = q_ref[...].astype(f32)
    keys = k_ref[...].astype(f32)
    values = v_ref[...].astype(f32)
    upstream = go_ref[...].astype(f32)
    gated = (keys * values).astype(bf16)
    cot = (upstream * query).astype(bf16)
    u_all = jnp.concatenate([prev_ref[...], gated], axis=0)
    c_all = jnp.concatenate([cot, next_ref[...]], axis=0)
    lane_group = lax.broadcasted_iota(jnp.int32, (1, LANES), 1) // GROUP
    windows = [u_all[b * FLEN:(b + 2) * FLEN] for b in range(blocks)]
    cots = [c_all[b * FLEN:(b + 1) * FLEN] for b in range(blocks + 1)]
    masks = [m_ref[b] for b in range(blocks + 1)]
    masks_t = [mt_ref[b] for b in range(blocks + 1)]
    masks_r = [mr_ref[b].astype(f32) for b in range(blocks)]
    flip = (lax.broadcasted_iota(jnp.int32, (FLEN, FLEN), 0)
            + lax.broadcasted_iota(jnp.int32, (FLEN, FLEN), 1) == FLEN - 1).astype(bf16)
    cots_r = [jnp.dot(flip, cots[b], preferred_element_type=f32).astype(bf16) for b in range(blocks)]
    mixed = [jnp.zeros((FLEN, LANES), f32) for _ in range(blocks)]
    cots_t = [c.astype(f32).T.astype(bf16) for c in cots]
    row_group = lax.broadcasted_iota(jnp.int32, (LANES, 1), 0) // GROUP
    own_t = [jnp.zeros((LANES, FLEN), f32) for _ in range(blocks)]
    spill_t = [jnp.zeros((LANES, FLEN), f32) for _ in range(blocks)]
    nt = (((1,), (1,)), ((), ()))
    sums = []
    for k in range(LANES // GROUP):
        prow = jnp.broadcast_to(fp_ref[k:k + 1, :], (FLEN, 2 * FLEN))
        taps = pltpu.roll(prow, 0, 1, stride=1, stride_axis=0).astype(bf16)
        in_group = lane_group == k
        in_rows = row_group == k
        acc = jnp.zeros((FLEN, 2 * FLEN), f32)
        for b in range(blocks + 1):
            group_cot_t = jnp.where(in_rows, cots_t[b], jnp.zeros_like(cots_t[b]))
            if b < blocks:
                operator = taps * masks[b]
                window = jnp.where(in_group, windows[b], jnp.zeros_like(windows[b]))
                mixed[b] = mixed[b] + jnp.dot(operator, window, preferred_element_type=f32)
                own_t[b] = own_t[b] + jnp.dot(group_cot_t, operator[:, FLEN:], preferred_element_type=f32)
                group_cot = jnp.where(in_group, cots_r[b], jnp.zeros_like(cots_r[b]))
                prods = lax.dot_general(group_cot, windows[b], nt, preferred_element_type=f32)
                acc = acc + prods * masks_r[b]
            if b > 0:
                lead = taps[:, :FLEN] * masks[b][:, :FLEN]
                spill_t[b - 1] = spill_t[b - 1] + jnp.dot(group_cot_t, lead, preferred_element_type=f32)
        skewed = pltpu.roll(acc, 0, 1, stride=1, stride_axis=0)
        sums.append(jnp.sum(skewed, axis=0, keepdims=True))
    raw_ref[0] = jnp.concatenate(sums, axis=0)
    mixed_all = jnp.concatenate(mixed, axis=0)
    back_all = jnp.concatenate([(own_t[b] + spill_t[b]).T for b in range(blocks)], axis=0)
    mo_ref[...] = (query * mixed_all).astype(bf16)
    gq_ref[...] = (upstream * mixed_all).astype(bf16)
    gk_ref[...] = (back_all * values).astype(bf16)
    gv_ref[...] = (back_all * keys).astype(bf16)


def grouped_conv(q2, k2, v2, g2, prev_tail, next_head, fp, fq, mask, mask_t, interpret=False):
    mask_r = mask[:-1, ::-1, :]
    rows, channels = q2.shape
    tiles = channels // LANES
    per_tile = LANES // GROUP
    nb = rows // FLEN
    tok = pl.BlockSpec((rows, LANES), lambda j: (0, j))
    halo = pl.BlockSpec((FLEN, LANES), lambda j: (0, j))
    filt = pl.BlockSpec((per_tile, 2 * FLEN), lambda j: (j, 0))
    mspec = pl.BlockSpec((nb + 1, FLEN, 2 * FLEN), lambda j: (0, 0, 0))
    mtspec = pl.BlockSpec((nb + 1, 2 * FLEN, FLEN), lambda j: (0, 0, 0))
    mrspec = pl.BlockSpec((nb, FLEN, 2 * FLEN), lambda j: (0, 0, 0))
    out_tok = jax.ShapeDtypeStruct((rows, channels), jnp.bfloat16)
    return pl.pallas_call(
        conv_kernel,
        grid=(tiles,),
        in_specs=[tok, tok, tok, tok, halo, halo, filt, filt, mspec, mtspec, mrspec],
        out_specs=[tok, tok, tok, tok, pl.BlockSpec((1, per_tile, 2 * FLEN), lambda j: (j, 0, 0))],
        out_shape=[out_tok, out_tok, out_tok, out_tok,
                   jax.ShapeDtypeStruct((tiles, per_tile, 2 * FLEN), jnp.float32)],
        interpret=interpret,
    )(q2, k2, v2, g2, prev_tail, next_head, fp, fq, mask, mask_t, mask_r)


def doc_masks(lengths, offset, rows):
    starts = jnp.cumsum(lengths) - lengths
    nb = rows // FLEN
    b_ids = jnp.arange(nb + 1, dtype=jnp.int32)[:, None]
    tpos = offset + b_ids * FLEN + jnp.arange(FLEN, dtype=jnp.int32)[None, :]
    doc_begin = jnp.max(jnp.where(starts[None, None, :] <= tpos[:, :, None], starts[None, None, :], 0), axis=2)
    rpos = offset + (b_ids - 1) * FLEN + jnp.arange(2 * FLEN, dtype=jnp.int32)[None, :]
    lag = jnp.arange(FLEN, dtype=jnp.int32)[:, None] + FLEN - jnp.arange(2 * FLEN, dtype=jnp.int32)[None, :]
    inside = (lag >= 0) & (lag < FLEN)
    mask = ((rpos[:, None, :] >= doc_begin[:, :, None]) & inside[None]).astype(jnp.bfloat16)
    return mask, mask.transpose(0, 2, 1)


def filter_rows(filters):
    taps = filters.astype(jnp.float32)
    groups = taps.shape[0]
    fp = jnp.concatenate([jnp.zeros((groups, 1), jnp.float32), taps[:, ::-1],
                          jnp.zeros((groups, FLEN - 1), jnp.float32)], axis=1)
    fq = jnp.concatenate([taps, jnp.zeros((groups, FLEN), jnp.float32)], axis=1)
    return fp, fq


def on_device(query_in, key_in, value_in, grad_out, seq_lengths, filters):
    f32, bf16 = jnp.float32, jnp.bfloat16
    q2, k2, v2, g2 = query_in[0], key_in[0], value_in[0], grad_out[0]
    rows = q2.shape[0]
    tail = (k2[rows - FLEN:].astype(f32) * v2[rows - FLEN:].astype(f32)).astype(bf16)
    head = (g2[:FLEN].astype(f32) * q2[:FLEN].astype(f32)).astype(bf16)
    prev_tail = passed_along(tail, "ctx", 1)
    next_head = passed_along(head, "ctx", -1)
    mask, mask_t = doc_masks(seq_lengths[0], lax.axis_index("ctx") * rows, rows)
    fp, fq = filter_rows(filters)
    mixed_out, grad_query, grad_key, grad_value, cols = grouped_conv(
        q2, k2, v2, g2, prev_tail, next_head, fp, fq, mask, mask_t)
    local_raw = cols.reshape(-1, 2 * FLEN)[:, 2 * FLEN - 1:FLEN - 1:-1]
    summed = doubling_sum(doubling_sum(local_raw, "dp"), "ctx")
    squares = doubling_sum(jnp.sum(summed * summed), "tensor")
    factor = jnp.minimum(1.0, math.sqrt(GROUPS * FLEN) / jnp.sqrt(squares))
    grad_filters = summed * factor
    return (mixed_out[None], grad_query[None], grad_key[None], grad_value[None], grad_filters)


def solution(mesh):
    tok = P("dp", "ctx", "tensor")
    in_specs = (tok, tok, tok, tok, P("dp", None), P("tensor", None))
    out_specs = (tok, tok, tok, tok, P("tensor", None))
    return jax.shard_map(
        on_device, mesh=mesh, in_specs=in_specs, out_specs=out_specs, check_vma=False
    )
```

```python
import math

import jax
import jax.numpy as jnp
from jax import lax
from jax.experimental import pallas as pl
from jax.experimental.pallas import tpu as pltpu
from jax.sharding import PartitionSpec as P

GROUP = 16
FLEN = 128
GROUPS = 512
LANES = 128


def passed_along(value, axis, steps):
    count = lax.axis_size(axis)
    initial, last = (max(0, -steps), min(count, count - steps))
    return lax.ppermute(value, axis, [(source, source + steps) for source in range(initial, last)])


def doubling_sum(value, axis):
    count = lax.axis_size(axis)
    step = 1
    while step < count:
        partner = lax.ppermute(value, axis, [(i, i ^ step) for i in range(count)])
        value = value + partner
        step *= 2
    return value


def conv_kernel(q_ref, k_ref, v_ref, go_ref, prev_ref, next_ref, fp_ref, fq_ref, m_ref, mt_ref, mr_ref,
                mo_ref, gq_ref, gk_ref, gv_ref, raw_ref):
    f32, bf16 = jnp.float32, jnp.bfloat16
    rows = q_ref.shape[0]
    blocks = rows // FLEN
    query = q_ref[...].astype(f32)
    keys = k_ref[...].astype(f32)
    values = v_ref[...].astype(f32)
    upstream = go_ref[...].astype(f32)
    gated = (keys * values).astype(bf16)
    cot = (upstream * query).astype(bf16)
    u_all = jnp.concatenate([prev_ref[...], gated], axis=0)
    c_all = jnp.concatenate([cot, next_ref[...]], axis=0)
    lane_group = lax.broadcasted_iota(jnp.int32, (1, LANES), 1) // GROUP
    windows = [u_all[b * FLEN:(b + 2) * FLEN] for b in range(blocks)]
    cots = [c_all[b * FLEN:(b + 1) * FLEN] for b in range(blocks + 1)]
    masks = [m_ref[b] for b in range(blocks + 1)]
    masks_t = [mt_ref[b] for b in range(blocks + 1)]
    masks_r = [mr_ref[b].astype(f32) for b in range(blocks)]
    flip = (lax.broadcasted_iota(jnp.int32, (FLEN, FLEN), 0)
            + lax.broadcasted_iota(jnp.int32, (FLEN, FLEN), 1) == FLEN - 1).astype(bf16)
    cots_r = [jnp.dot(flip, cots[b], preferred_element_type=f32).astype(bf16) for b in range(blocks)]
    cots_t = [c.astype(f32).T.astype(bf16) for c in cots]
    windows_t = [w.astype(f32).T.astype(bf16) for w in windows]
    mixed_t = [[] for _ in range(blocks)]
    own_t = [[] for _ in range(blocks)]
    spill_t = [[] for _ in range(blocks)]
    nt = (((1,), (1,)), ((), ()))
    sums = []
    for k in range(LANES // GROUP):
        prow = jnp.broadcast_to(fp_ref[k:k + 1, :], (FLEN, 2 * FLEN))
        taps = pltpu.roll(prow, 0, 1, stride=1, stride_axis=0).astype(bf16)
        rows_k = slice(k * GROUP, (k + 1) * GROUP)
        in_group = lane_group == k
        acc = jnp.zeros((FLEN, 2 * FLEN), f32)
        for b in range(blocks + 1):
            group_cot_t = cots_t[b][rows_k]
            if b < blocks:
                operator = taps * masks[b]
                mixed_t[b].append(lax.dot_general(windows_t[b][rows_k], operator, nt, preferred_element_type=f32))
                own_t[b].append(jnp.dot(group_cot_t, operator[:, FLEN:], preferred_element_type=f32))
                group_cot = jnp.where(in_group, cots_r[b], jnp.zeros_like(cots_r[b]))
                prods = lax.dot_general(group_cot, windows[b], nt, preferred_element_type=f32)
                acc = acc + prods * masks_r[b]
            if b > 0:
                lead = taps[:, :FLEN] * masks[b][:, :FLEN]
                spill_t[b - 1].append(jnp.dot(group_cot_t, lead, preferred_element_type=f32))
        skewed = pltpu.roll(acc, 0, 1, stride=1, stride_axis=0)
        sums.append(jnp.sum(skewed, axis=0, keepdims=True))
    raw_ref[0] = jnp.concatenate(sums, axis=0)
    mixed_all = jnp.concatenate([jnp.concatenate(m, axis=0).T for m in mixed_t], axis=0)
    back_all = jnp.concatenate(
        [(jnp.concatenate(own_t[b], axis=0) + jnp.concatenate(spill_t[b], axis=0)).T for b in range(blocks)], axis=0)
    mo_ref[...] = (query * mixed_all).astype(bf16)
    gq_ref[...] = (upstream * mixed_all).astype(bf16)
    gk_ref[...] = (back_all * values).astype(bf16)
    gv_ref[...] = (back_all * keys).astype(bf16)


def grouped_conv(q2, k2, v2, g2, prev_tail, next_head, fp, fq, mask, mask_t, interpret=False):
    mask_r = mask[:-1, ::-1, :]
    rows, channels = q2.shape
    tiles = channels // LANES
    per_tile = LANES // GROUP
    nb = rows // FLEN
    tok = pl.BlockSpec((rows, LANES), lambda j: (0, j))
    halo = pl.BlockSpec((FLEN, LANES), lambda j: (0, j))
    filt = pl.BlockSpec((per_tile, 2 * FLEN), lambda j: (j, 0))
    mspec = pl.BlockSpec((nb + 1, FLEN, 2 * FLEN), lambda j: (0, 0, 0))
    mtspec = pl.BlockSpec((nb + 1, 2 * FLEN, FLEN), lambda j: (0, 0, 0))
    mrspec = pl.BlockSpec((nb, FLEN, 2 * FLEN), lambda j: (0, 0, 0))
    out_tok = jax.ShapeDtypeStruct((rows, channels), jnp.bfloat16)
    return pl.pallas_call(
        conv_kernel,
        grid=(tiles,),
        in_specs=[tok, tok, tok, tok, halo, halo, filt, filt, mspec, mtspec, mrspec],
        out_specs=[tok, tok, tok, tok, pl.BlockSpec((1, per_tile, 2 * FLEN), lambda j: (j, 0, 0))],
        out_shape=[out_tok, out_tok, out_tok, out_tok,
                   jax.ShapeDtypeStruct((tiles, per_tile, 2 * FLEN), jnp.float32)],
        interpret=interpret,
    )(q2, k2, v2, g2, prev_tail, next_head, fp, fq, mask, mask_t, mask_r)


def doc_masks(lengths, offset, rows):
    starts = jnp.cumsum(lengths) - lengths
    nb = rows // FLEN
    b_ids = jnp.arange(nb + 1, dtype=jnp.int32)[:, None]
    tpos = offset + b_ids * FLEN + jnp.arange(FLEN, dtype=jnp.int32)[None, :]
    doc_begin = jnp.max(jnp.where(starts[None, None, :] <= tpos[:, :, None], starts[None, None, :], 0), axis=2)
    rpos = offset + (b_ids - 1) * FLEN + jnp.arange(2 * FLEN, dtype=jnp.int32)[None, :]
    lag = jnp.arange(FLEN, dtype=jnp.int32)[:, None] + FLEN - jnp.arange(2 * FLEN, dtype=jnp.int32)[None, :]
    inside = (lag >= 0) & (lag < FLEN)
    mask = ((rpos[:, None, :] >= doc_begin[:, :, None]) & inside[None]).astype(jnp.bfloat16)
    return mask, mask.transpose(0, 2, 1)


def filter_rows(filters):
    taps = filters.astype(jnp.float32)
    groups = taps.shape[0]
    fp = jnp.concatenate([jnp.zeros((groups, 1), jnp.float32), taps[:, ::-1],
                          jnp.zeros((groups, FLEN - 1), jnp.float32)], axis=1)
    fq = jnp.concatenate([taps, jnp.zeros((groups, FLEN), jnp.float32)], axis=1)
    return fp, fq


def on_device(query_in, key_in, value_in, grad_out, seq_lengths, filters):
    f32, bf16 = jnp.float32, jnp.bfloat16
    q2, k2, v2, g2 = query_in[0], key_in[0], value_in[0], grad_out[0]
    rows = q2.shape[0]
    tail = (k2[rows - FLEN:].astype(f32) * v2[rows - FLEN:].astype(f32)).astype(bf16)
    head = (g2[:FLEN].astype(f32) * q2[:FLEN].astype(f32)).astype(bf16)
    prev_tail = passed_along(tail, "ctx", 1)
    next_head = passed_along(head, "ctx", -1)
    mask, mask_t = doc_masks(seq_lengths[0], lax.axis_index("ctx") * rows, rows)
    fp, fq = filter_rows(filters)
    mixed_out, grad_query, grad_key, grad_value, cols = grouped_conv(
        q2, k2, v2, g2, prev_tail, next_head, fp, fq, mask, mask_t)
    local_raw = cols.reshape(-1, 2 * FLEN)[:, 2 * FLEN - 1:FLEN - 1:-1]
    summed = doubling_sum(doubling_sum(local_raw, "dp"), "ctx")
    squares = doubling_sum(jnp.sum(summed * summed), "tensor")
    factor = jnp.minimum(1.0, math.sqrt(GROUPS * FLEN) / jnp.sqrt(squares))
    grad_filters = summed * factor
    return (mixed_out[None], grad_query[None], grad_key[None], grad_value[None], grad_filters)


def solution(mesh):
    tok = P("dp", "ctx", "tensor")
    in_specs = (tok, tok, tok, tok, P("dp", None), P("tensor", None))
    out_specs = (tok, tok, tok, tok, P("tensor", None))
    return jax.shard_map(
        on_device, mesh=mesh, in_specs=in_specs, out_specs=out_specs, check_vma=False
    )
```

```python
import functools
import math

import jax
import jax.numpy as jnp
from jax import lax
from jax.experimental import pallas as pl
from jax.experimental.pallas import tpu as pltpu
from jax.sharding import PartitionSpec as P

GROUP = 16
FLEN = 128
GROUPS = 512
LANES = 128


def passed_along(value, axis, steps):
    count = lax.axis_size(axis)
    initial, last = (max(0, -steps), min(count, count - steps))
    return lax.ppermute(value, axis, [(source, source + steps) for source in range(initial, last)])


def doubling_sum(value, axis):
    count = lax.axis_size(axis)
    step = 1
    while step < count:
        partner = lax.ppermute(value, axis, [(i, i ^ step) for i in range(count)])
        value = value + partner
        step *= 2
    return value


def conv_kernel(q_ref, k_ref, v_ref, go_ref, prev_ref, next_ref, fp_ref, fq_ref, m_ref, mt_ref, mr_ref, *refs, extra):
    mo_ref, gq_ref, gk_ref, gv_ref, raw_ref = refs[extra:]
    f32, bf16 = jnp.float32, jnp.bfloat16
    rows = q_ref.shape[0]
    blocks = rows // FLEN
    query = q_ref[...].astype(f32)
    keys = k_ref[...].astype(f32)
    values = v_ref[...].astype(f32)
    upstream = go_ref[...].astype(f32)
    gated = (keys * values).astype(bf16)
    cot = (upstream * query).astype(bf16)
    u_all = jnp.concatenate([prev_ref[...], gated], axis=0)
    c_all = jnp.concatenate([cot, next_ref[...]], axis=0)
    lane_group = lax.broadcasted_iota(jnp.int32, (1, LANES), 1) // GROUP
    windows = [u_all[b * FLEN:(b + 2) * FLEN] for b in range(blocks)]
    cots = [c_all[b * FLEN:(b + 1) * FLEN] for b in range(blocks + 1)]
    masks = [m_ref[b] for b in range(blocks + 1)]
    masks_t = [mt_ref[b] for b in range(blocks + 1)]
    masks_r = [mr_ref[b].astype(f32) for b in range(blocks)]
    flip = (lax.broadcasted_iota(jnp.int32, (FLEN, FLEN), 0)
            + lax.broadcasted_iota(jnp.int32, (FLEN, FLEN), 1) == FLEN - 1).astype(bf16)
    cots_r = [jnp.dot(flip, cots[b], preferred_element_type=f32).astype(bf16) for b in range(blocks)]
    cots_t = [c.astype(f32).T.astype(bf16) for c in cots]
    windows_t = [w.astype(f32).T.astype(bf16) for w in windows]
    mixed_t = [[] for _ in range(blocks)]
    own_t = [[] for _ in range(blocks)]
    spill_t = [[] for _ in range(blocks)]
    nt = (((1,), (1,)), ((), ()))
    sums = []
    for k in range(LANES // GROUP):
        prow = jnp.broadcast_to(fp_ref[k:k + 1, :], (FLEN, 2 * FLEN))
        taps = pltpu.roll(prow, 0, 1, stride=1, stride_axis=0).astype(bf16)
        rows_k = slice(k * GROUP, (k + 1) * GROUP)
        in_group = lane_group == k
        acc = jnp.zeros((FLEN, 2 * FLEN), f32)
        for b in range(blocks + 1):
            group_cot_t = cots_t[b][rows_k]
            if b < blocks:
                operator = taps * masks[b]
                mixed_t[b].append(lax.dot_general(windows_t[b][rows_k], operator, nt, preferred_element_type=f32))
                own_t[b].append(jnp.dot(group_cot_t, operator[:, FLEN:], preferred_element_type=f32))
                group_cot = jnp.where(in_group, cots_r[b], jnp.zeros_like(cots_r[b]))
                prods = lax.dot_general(group_cot, windows[b], nt, preferred_element_type=f32)
                acc = acc + prods * masks_r[b]
            if b > 0:
                lead = taps[:, :FLEN] * masks[b][:, :FLEN]
                spill_t[b - 1].append(jnp.dot(group_cot_t, lead, preferred_element_type=f32))
        skewed = pltpu.roll(acc, 0, 1, stride=1, stride_axis=0)
        sums.append(jnp.sum(skewed, axis=0, keepdims=True))
    raw_ref[0] = jnp.concatenate(sums, axis=0)
    mixed_all = jnp.concatenate([jnp.concatenate(m, axis=0).T for m in mixed_t], axis=0)
    back_all = jnp.concatenate(
        [(jnp.concatenate(own_t[b], axis=0) + jnp.concatenate(spill_t[b], axis=0)).T for b in range(blocks)], axis=0)
    mo_ref[...] = (query * mixed_all).astype(bf16)
    gq_ref[...] = (upstream * mixed_all).astype(bf16)
    gk_ref[...] = (back_all * values).astype(bf16)
    gv_ref[...] = (back_all * keys).astype(bf16)


def grouped_conv(q2, k2, v2, g2, prev_tail, next_head, fp, fq, mask, mask_t, first=0, outs=None, interpret=False):
    mask_r = mask[:-1, ::-1, :]
    rows, channels = q2.shape
    tiles = prev_tail.shape[1] // LANES
    per_tile = LANES // GROUP
    nb = rows // FLEN
    tok = pl.BlockSpec((rows, LANES), lambda j: (0, j + first))
    halo = pl.BlockSpec((FLEN, LANES), lambda j: (0, j))
    filt = pl.BlockSpec((per_tile, 2 * FLEN), lambda j: (j + first, 0))
    mspec = pl.BlockSpec((nb + 1, FLEN, 2 * FLEN), lambda j: (0, 0, 0))
    mtspec = pl.BlockSpec((nb + 1, 2 * FLEN, FLEN), lambda j: (0, 0, 0))
    mrspec = pl.BlockSpec((nb, FLEN, 2 * FLEN), lambda j: (0, 0, 0))
    in_specs = [tok, tok, tok, tok, halo, halo, filt, filt, mspec, mtspec, mrspec]
    operands = [q2, k2, v2, g2, prev_tail, next_head, fp, fq, mask, mask_t, mask_r]
    aliases = {}
    if outs is not None:
        for i, o in enumerate(outs):
            aliases[len(operands)] = i
            operands.append(o)
            in_specs.append(pl.BlockSpec(memory_space=pl.ANY))
    out_tok = jax.ShapeDtypeStruct((rows, channels), jnp.bfloat16)
    return pl.pallas_call(
        functools.partial(conv_kernel, extra=len(aliases)),
        grid=(tiles,),
        in_specs=in_specs,
        out_specs=[tok, tok, tok, tok, pl.BlockSpec((1, per_tile, 2 * FLEN), lambda j: (j, 0, 0))],
        out_shape=[out_tok, out_tok, out_tok, out_tok,
                   jax.ShapeDtypeStruct((tiles, per_tile, 2 * FLEN), jnp.float32)],
        input_output_aliases=aliases,
        interpret=interpret,
    )(*operands)


def doc_masks(lengths, offset, rows):
    starts = jnp.cumsum(lengths) - lengths
    nb = rows // FLEN
    b_ids = jnp.arange(nb + 1, dtype=jnp.int32)[:, None]
    tpos = offset + b_ids * FLEN + jnp.arange(FLEN, dtype=jnp.int32)[None, :]
    doc_begin = jnp.max(jnp.where(starts[None, None, :] <= tpos[:, :, None], starts[None, None, :], 0), axis=2)
    rpos = offset + (b_ids - 1) * FLEN + jnp.arange(2 * FLEN, dtype=jnp.int32)[None, :]
    lag = jnp.arange(FLEN, dtype=jnp.int32)[:, None] + FLEN - jnp.arange(2 * FLEN, dtype=jnp.int32)[None, :]
    inside = (lag >= 0) & (lag < FLEN)
    mask = ((rpos[:, None, :] >= doc_begin[:, :, None]) & inside[None]).astype(jnp.bfloat16)
    return mask, mask.transpose(0, 2, 1)


def filter_rows(filters):
    taps = filters.astype(jnp.float32)
    groups = taps.shape[0]
    fp = jnp.concatenate([jnp.zeros((groups, 1), jnp.float32), taps[:, ::-1],
                          jnp.zeros((groups, FLEN - 1), jnp.float32)], axis=1)
    fq = jnp.concatenate([taps, jnp.zeros((groups, FLEN), jnp.float32)], axis=1)
    return fp, fq


def on_device(query_in, key_in, value_in, grad_out, seq_lengths, filters):
    f32, bf16 = jnp.float32, jnp.bfloat16
    q2, k2, v2, g2 = query_in[0], key_in[0], value_in[0], grad_out[0]
    rows, channels = q2.shape
    tail = (k2[rows - FLEN:].astype(f32) * v2[rows - FLEN:].astype(f32)).astype(bf16)
    head = (g2[:FLEN].astype(f32) * q2[:FLEN].astype(f32)).astype(bf16)
    half = channels // 2
    prev_tails = [passed_along(tail[:, :half], "ctx", 1), passed_along(tail[:, half:], "ctx", 1)]
    next_heads = [passed_along(head[:, :half], "ctx", -1), passed_along(head[:, half:], "ctx", -1)]
    mask, mask_t = doc_masks(seq_lengths[0], lax.axis_index("ctx") * rows, rows)
    fp, fq = filter_rows(filters)
    outs = None
    parts = []
    for p in range(2):
        result = grouped_conv(q2, k2, v2, g2, prev_tails[p], next_heads[p], fp, fq, mask, mask_t,
                              first=p * (half // LANES), outs=outs)
        outs = result[:4]
        parts.append(result[4])
    mixed_out, grad_query, grad_key, grad_value = outs
    cols = jnp.concatenate(parts, axis=0)
    local_raw = cols.reshape(-1, 2 * FLEN)[:, 2 * FLEN - 1:FLEN - 1:-1]
    summed = doubling_sum(doubling_sum(local_raw, "dp"), "ctx")
    squares = doubling_sum(jnp.sum(summed * summed), "tensor")
    factor = jnp.minimum(1.0, math.sqrt(GROUPS * FLEN) / jnp.sqrt(squares))
    grad_filters = summed * factor
    return (mixed_out[None], grad_query[None], grad_key[None], grad_value[None], grad_filters)


def solution(mesh):
    tok = P("dp", "ctx", "tensor")
    in_specs = (tok, tok, tok, tok, P("dp", None), P("tensor", None))
    out_specs = (tok, tok, tok, tok, P("tensor", None))
    return jax.shard_map(
        on_device, mesh=mesh, in_specs=in_specs, out_specs=out_specs, check_vma=False
    )
```

```python
import math

import jax
import jax.numpy as jnp
from jax import lax
from jax.experimental import pallas as pl
from jax.experimental.pallas import tpu as pltpu
from jax.sharding import PartitionSpec as P

GROUP = 16
FLEN = 128
GROUPS = 512
LANES = 128


def passed_along(value, axis, steps):
    count = lax.axis_size(axis)
    initial, last = (max(0, -steps), min(count, count - steps))
    return lax.ppermute(value, axis, [(source, source + steps) for source in range(initial, last)])


def doubling_sum(value, axis, masks):
    count = lax.axis_size(axis)
    for mask in masks:
        partner = lax.ppermute(value, axis, [(i, i ^ mask) for i in range(count)])
        value = value + partner
    return value


def conv_kernel(q_ref, k_ref, v_ref, go_ref, prev_ref, next_ref, fp_ref, fq_ref, m_ref, mt_ref, mr_ref,
                mo_ref, gq_ref, gk_ref, gv_ref, raw_ref):
    f32, bf16 = jnp.float32, jnp.bfloat16
    rows = q_ref.shape[0]
    blocks = rows // FLEN
    query = q_ref[...].astype(f32)
    keys = k_ref[...].astype(f32)
    values = v_ref[...].astype(f32)
    upstream = go_ref[...].astype(f32)
    gated = (keys * values).astype(bf16)
    cot = (upstream * query).astype(bf16)
    u_all = jnp.concatenate([prev_ref[...], gated], axis=0)
    c_all = jnp.concatenate([cot, next_ref[...]], axis=0)
    lane_group = lax.broadcasted_iota(jnp.int32, (1, LANES), 1) // GROUP
    windows = [u_all[b * FLEN:(b + 2) * FLEN] for b in range(blocks)]
    cots = [c_all[b * FLEN:(b + 1) * FLEN] for b in range(blocks + 1)]
    masks = [m_ref[b] for b in range(blocks + 1)]
    masks_t = [mt_ref[b] for b in range(blocks + 1)]
    masks_r = [mr_ref[b].astype(f32) for b in range(blocks)]
    flip = (lax.broadcasted_iota(jnp.int32, (FLEN, FLEN), 0)
            + lax.broadcasted_iota(jnp.int32, (FLEN, FLEN), 1) == FLEN - 1).astype(bf16)
    cots_r = [jnp.dot(flip, cots[b], preferred_element_type=f32).astype(bf16) for b in range(blocks)]
    cots_t = [c.astype(f32).T.astype(bf16) for c in cots]
    windows_t = [w.astype(f32).T.astype(bf16) for w in windows]
    mixed_t = [[] for _ in range(blocks)]
    own_t = [[] for _ in range(blocks)]
    spill_t = [[] for _ in range(blocks)]
    nt = (((1,), (1,)), ((), ()))
    sums = []
    for k in range(LANES // GROUP):
        prow = jnp.broadcast_to(fp_ref[k:k + 1, :], (FLEN, 2 * FLEN))
        taps = pltpu.roll(prow, 0, 1, stride=1, stride_axis=0).astype(bf16)
        rows_k = slice(k * GROUP, (k + 1) * GROUP)
        in_group = lane_group == k
        acc = jnp.zeros((FLEN, 2 * FLEN), f32)
        for b in range(blocks + 1):
            group_cot_t = cots_t[b][rows_k]
            if b < blocks:
                operator = taps * masks[b]
                mixed_t[b].append(lax.dot_general(windows_t[b][rows_k], operator, nt, preferred_element_type=f32))
                own_t[b].append(jnp.dot(group_cot_t, operator[:, FLEN:], preferred_element_type=f32))
                group_cot = jnp.where(in_group, cots_r[b], jnp.zeros_like(cots_r[b]))
                prods = lax.dot_general(group_cot, windows[b], nt, preferred_element_type=f32)
                acc = acc + prods * masks_r[b]
            if b > 0:
                lead = taps[:, :FLEN] * masks[b][:, :FLEN]
                spill_t[b - 1].append(jnp.dot(group_cot_t, lead, preferred_element_type=f32))
        skewed = pltpu.roll(acc, 0, 1, stride=1, stride_axis=0)
        sums.append(jnp.sum(skewed, axis=0, keepdims=True))
    raw_ref[0] = jnp.concatenate(sums, axis=0)
    mixed_all = jnp.concatenate([jnp.concatenate(m, axis=0).T for m in mixed_t], axis=0)
    back_all = jnp.concatenate(
        [(jnp.concatenate(own_t[b], axis=0) + jnp.concatenate(spill_t[b], axis=0)).T for b in range(blocks)], axis=0)
    mo_ref[...] = (query * mixed_all).astype(bf16)
    gq_ref[...] = (upstream * mixed_all).astype(bf16)
    gk_ref[...] = (back_all * values).astype(bf16)
    gv_ref[...] = (back_all * keys).astype(bf16)


def grouped_conv(q2, k2, v2, g2, prev_tail, next_head, fp, fq, mask, mask_t, interpret=False):
    mask_r = mask[:-1, ::-1, :]
    rows, channels = q2.shape
    tiles = channels // LANES
    per_tile = LANES // GROUP
    nb = rows // FLEN
    tok = pl.BlockSpec((rows, LANES), lambda j: (0, j))
    halo = pl.BlockSpec((FLEN, LANES), lambda j: (0, j))
    filt = pl.BlockSpec((per_tile, 2 * FLEN), lambda j: (j, 0))
    mspec = pl.BlockSpec((nb + 1, FLEN, 2 * FLEN), lambda j: (0, 0, 0))
    mtspec = pl.BlockSpec((nb + 1, 2 * FLEN, FLEN), lambda j: (0, 0, 0))
    mrspec = pl.BlockSpec((nb, FLEN, 2 * FLEN), lambda j: (0, 0, 0))
    out_tok = jax.ShapeDtypeStruct((rows, channels), jnp.bfloat16)
    return pl.pallas_call(
        conv_kernel,
        grid=(tiles,),
        in_specs=[tok, tok, tok, tok, halo, halo, filt, filt, mspec, mtspec, mrspec],
        out_specs=[tok, tok, tok, tok, pl.BlockSpec((1, per_tile, 2 * FLEN), lambda j: (j, 0, 0))],
        out_shape=[out_tok, out_tok, out_tok, out_tok,
                   jax.ShapeDtypeStruct((tiles, per_tile, 2 * FLEN), jnp.float32)],
        interpret=interpret,
    )(q2, k2, v2, g2, prev_tail, next_head, fp, fq, mask, mask_t, mask_r)


def doc_masks(lengths, offset, rows):
    starts = jnp.cumsum(lengths) - lengths
    nb = rows // FLEN
    b_ids = jnp.arange(nb + 1, dtype=jnp.int32)[:, None]
    tpos = offset + b_ids * FLEN + jnp.arange(FLEN, dtype=jnp.int32)[None, :]
    doc_begin = jnp.max(jnp.where(starts[None, None, :] <= tpos[:, :, None], starts[None, None, :], 0), axis=2)
    rpos = offset + (b_ids - 1) * FLEN + jnp.arange(2 * FLEN, dtype=jnp.int32)[None, :]
    lag = jnp.arange(FLEN, dtype=jnp.int32)[:, None] + FLEN - jnp.arange(2 * FLEN, dtype=jnp.int32)[None, :]
    inside = (lag >= 0) & (lag < FLEN)
    mask = ((rpos[:, None, :] >= doc_begin[:, :, None]) & inside[None]).astype(jnp.bfloat16)
    return mask, mask.transpose(0, 2, 1)


def filter_rows(filters):
    taps = filters.astype(jnp.float32)
    groups = taps.shape[0]
    fp = jnp.concatenate([jnp.zeros((groups, 1), jnp.float32), taps[:, ::-1],
                          jnp.zeros((groups, FLEN - 1), jnp.float32)], axis=1)
    fq = jnp.concatenate([taps, jnp.zeros((groups, FLEN), jnp.float32)], axis=1)
    return fp, fq


def mirror_masks(count):
    masks, width = [], 1
    while width < count:
        masks.append(2 * width - 1)
        width *= 2
    return masks


def ctx_masks():
    inner = 8 if lax.axis_size("ctx") % 8 == 0 else 1
    outer = lax.axis_size("ctx") // inner
    low = [1, 2, 7][: inner.bit_length() - 1]
    return low + [m * inner for m in mirror_masks(outer)]


def on_device(query_in, key_in, value_in, grad_out, seq_lengths, filters):
    f32, bf16 = jnp.float32, jnp.bfloat16
    q2, k2, v2, g2 = query_in[0], key_in[0], value_in[0], grad_out[0]
    rows = q2.shape[0]
    tail = (k2[rows - FLEN:].astype(f32) * v2[rows - FLEN:].astype(f32)).astype(bf16)
    head = (g2[:FLEN].astype(f32) * q2[:FLEN].astype(f32)).astype(bf16)
    prev_tail = passed_along(tail, "ctx", 1)
    next_head = passed_along(head, "ctx", -1)
    mask, mask_t = doc_masks(seq_lengths[0], lax.axis_index("ctx") * rows, rows)
    fp, fq = filter_rows(filters)
    mixed_out, grad_query, grad_key, grad_value, cols = grouped_conv(
        q2, k2, v2, g2, prev_tail, next_head, fp, fq, mask, mask_t)
    local_raw = cols.reshape(-1, 2 * FLEN)[:, 2 * FLEN - 1:FLEN - 1:-1]
    summed = doubling_sum(doubling_sum(local_raw, "dp", mirror_masks(lax.axis_size("dp"))), "ctx", ctx_masks())
    squares = doubling_sum(jnp.sum(summed * summed), "tensor", mirror_masks(lax.axis_size("tensor")))
    factor = jnp.minimum(1.0, math.sqrt(GROUPS * FLEN) / jnp.sqrt(squares))
    grad_filters = summed * factor
    return (mixed_out[None], grad_query[None], grad_key[None], grad_value[None], grad_filters)


def solution(mesh):
    tok = P("dp", "ctx", "tensor")
    in_specs = (tok, tok, tok, tok, P("dp", None), P("tensor", None))
    out_specs = (tok, tok, tok, tok, P("tensor", None))
    return jax.shard_map(
        on_device, mesh=mesh, in_specs=in_specs, out_specs=out_specs, check_vma=False
    )
```

```python
import math

import jax
import jax.numpy as jnp
from jax import lax
from jax.experimental import pallas as pl
from jax.experimental.pallas import tpu as pltpu
from jax.sharding import PartitionSpec as P

GROUP = 16
FLEN = 128
GROUPS = 512
LANES = 128


def passed_along(value, axis, steps):
    count = lax.axis_size(axis)
    initial, last = (max(0, -steps), min(count, count - steps))
    return lax.ppermute(value, axis, [(source, source + steps) for source in range(initial, last)])


def doubling_sum(value, axis, masks):
    count = lax.axis_size(axis)
    for mask in masks:
        partner = lax.ppermute(value, axis, [(i, i ^ mask) for i in range(count)])
        value = value + partner
    return value


def conv_kernel(q_ref, k_ref, v_ref, go_ref, prev_ref, next_ref, fp_ref, fq_ref, m_ref, mt_ref, mr_ref,
                mo_ref, gq_ref, gk_ref, gv_ref, raw_ref):
    f32, bf16 = jnp.float32, jnp.bfloat16
    rows = q_ref.shape[0]
    blocks = rows // FLEN
    query = q_ref[...].astype(f32)
    keys = k_ref[...].astype(f32)
    values = v_ref[...].astype(f32)
    upstream = go_ref[...].astype(f32)
    gated = (keys * values).astype(bf16)
    cot = (upstream * query).astype(bf16)
    u_all = jnp.concatenate([prev_ref[...], gated], axis=0)
    c_all = jnp.concatenate([cot, next_ref[...]], axis=0)
    lane_group = lax.broadcasted_iota(jnp.int32, (1, LANES), 1) // GROUP
    windows = [u_all[b * FLEN:(b + 2) * FLEN] for b in range(blocks)]
    cots = [c_all[b * FLEN:(b + 1) * FLEN] for b in range(blocks + 1)]
    masks = [m_ref[b] for b in range(blocks + 1)]
    masks_t = [mt_ref[b] for b in range(blocks + 1)]
    masks_r = [mr_ref[b].astype(f32) for b in range(blocks)]
    flip = (lax.broadcasted_iota(jnp.int32, (FLEN, FLEN), 0)
            + lax.broadcasted_iota(jnp.int32, (FLEN, FLEN), 1) == FLEN - 1).astype(bf16)
    cots_r = [jnp.dot(flip, cots[b], preferred_element_type=f32).astype(bf16) for b in range(blocks)]
    cots_t = [c.astype(f32).T.astype(bf16) for c in cots]
    windows_t = [w.astype(f32).T.astype(bf16) for w in windows]
    mixed_t = [[] for _ in range(blocks)]
    own_t = [[] for _ in range(blocks)]
    spill_t = [[] for _ in range(blocks)]
    nt = (((1,), (1,)), ((), ()))
    sums = []
    for k in range(LANES // GROUP):
        prow = jnp.broadcast_to(fp_ref[k:k + 1, :], (FLEN, 2 * FLEN))
        taps = pltpu.roll(prow, 0, 1, stride=1, stride_axis=0).astype(bf16)
        rows_k = slice(k * GROUP, (k + 1) * GROUP)
        in_group = lane_group == k
        acc = jnp.zeros((FLEN, 2 * FLEN), f32)
        for b in range(blocks + 1):
            group_cot_t = cots_t[b][rows_k]
            if b < blocks:
                operator = taps * masks[b]
                mixed_t[b].append(lax.dot_general(windows_t[b][rows_k], operator, nt, preferred_element_type=f32))
                own_t[b].append(jnp.dot(group_cot_t, operator[:, FLEN:], preferred_element_type=f32))
                group_cot = jnp.where(in_group, cots_r[b], jnp.zeros_like(cots_r[b]))
                prods = lax.dot_general(group_cot, windows[b], nt, preferred_element_type=f32)
                acc = acc + prods * masks_r[b]
            if b > 0:
                lead = taps[:, :FLEN] * masks[b][:, :FLEN]
                spill_t[b - 1].append(jnp.dot(group_cot_t, lead, preferred_element_type=f32))
        skewed = pltpu.roll(acc, 0, 1, stride=1, stride_axis=0)
        sums.append(jnp.sum(skewed, axis=0, keepdims=True))
    raw_ref[0] = jnp.concatenate(sums, axis=0)
    mixed_all = jnp.concatenate([jnp.concatenate(m, axis=0).T for m in mixed_t], axis=0)
    back_all = jnp.concatenate(
        [(jnp.concatenate(own_t[b], axis=0) + jnp.concatenate(spill_t[b], axis=0)).T for b in range(blocks)], axis=0)
    mo_ref[...] = (query * mixed_all).astype(bf16)
    gq_ref[...] = (upstream * mixed_all).astype(bf16)
    gk_ref[...] = (back_all * values).astype(bf16)
    gv_ref[...] = (back_all * keys).astype(bf16)


def grouped_conv(q2, k2, v2, g2, prev_tail, next_head, fp, fq, mask, mask_t, interpret=False):
    mask_r = mask[:-1, ::-1, :]
    rows, channels = q2.shape
    tiles = channels // LANES
    per_tile = LANES // GROUP
    nb = rows // FLEN
    tok = pl.BlockSpec((rows, LANES), lambda j: (0, j))
    halo = pl.BlockSpec((FLEN, LANES), lambda j: (0, j))
    filt = pl.BlockSpec((per_tile, 2 * FLEN), lambda j: (j, 0))
    mspec = pl.BlockSpec((nb + 1, FLEN, 2 * FLEN), lambda j: (0, 0, 0))
    mtspec = pl.BlockSpec((nb + 1, 2 * FLEN, FLEN), lambda j: (0, 0, 0))
    mrspec = pl.BlockSpec((nb, FLEN, 2 * FLEN), lambda j: (0, 0, 0))
    out_tok = jax.ShapeDtypeStruct((rows, channels), jnp.bfloat16)
    return pl.pallas_call(
        conv_kernel,
        grid=(tiles,),
        in_specs=[tok, tok, tok, tok, halo, halo, filt, filt, mspec, mtspec, mrspec],
        out_specs=[tok, tok, tok, tok, pl.BlockSpec((1, per_tile, 2 * FLEN), lambda j: (j, 0, 0))],
        out_shape=[out_tok, out_tok, out_tok, out_tok,
                   jax.ShapeDtypeStruct((tiles, per_tile, 2 * FLEN), jnp.float32)],
        interpret=interpret,
    )(q2, k2, v2, g2, prev_tail, next_head, fp, fq, mask, mask_t, mask_r)


def doc_masks(lengths, offset, rows):
    starts = jnp.cumsum(lengths) - lengths
    nb = rows // FLEN
    b_ids = jnp.arange(nb + 1, dtype=jnp.int32)[:, None]
    tpos = offset + b_ids * FLEN + jnp.arange(FLEN, dtype=jnp.int32)[None, :]
    doc_begin = jnp.max(jnp.where(starts[None, None, :] <= tpos[:, :, None], starts[None, None, :], 0), axis=2)
    rpos = offset + (b_ids - 1) * FLEN + jnp.arange(2 * FLEN, dtype=jnp.int32)[None, :]
    lag = jnp.arange(FLEN, dtype=jnp.int32)[:, None] + FLEN - jnp.arange(2 * FLEN, dtype=jnp.int32)[None, :]
    inside = (lag >= 0) & (lag < FLEN)
    mask = ((rpos[:, None, :] >= doc_begin[:, :, None]) & inside[None]).astype(jnp.bfloat16)
    return mask, mask.transpose(0, 2, 1)


def filter_rows(filters):
    taps = filters.astype(jnp.float32)
    groups = taps.shape[0]
    fp = jnp.concatenate([jnp.zeros((groups, 1), jnp.float32), taps[:, ::-1],
                          jnp.zeros((groups, FLEN - 1), jnp.float32)], axis=1)
    fq = jnp.concatenate([taps, jnp.zeros((groups, FLEN), jnp.float32)], axis=1)
    return fp, fq


def mirror_masks(count):
    masks, width = [], 1
    while width < count:
        masks.append(2 * width - 1)
        width *= 2
    return masks


def ctx_masks():
    inner = 8 if lax.axis_size("ctx") % 8 == 0 else 1
    outer = lax.axis_size("ctx") // inner
    low = [1, 2, 6][: inner.bit_length() - 1]
    return low + [m * inner for m in mirror_masks(outer)]


def on_device(query_in, key_in, value_in, grad_out, seq_lengths, filters):
    f32, bf16 = jnp.float32, jnp.bfloat16
    q2, k2, v2, g2 = query_in[0], key_in[0], value_in[0], grad_out[0]
    rows = q2.shape[0]
    tail = (k2[rows - FLEN:].astype(f32) * v2[rows - FLEN:].astype(f32)).astype(bf16)
    head = (g2[:FLEN].astype(f32) * q2[:FLEN].astype(f32)).astype(bf16)
    prev_tail = passed_along(tail, "ctx", 1)
    next_head = passed_along(head, "ctx", -1)
    mask, mask_t = doc_masks(seq_lengths[0], lax.axis_index("ctx") * rows, rows)
    fp, fq = filter_rows(filters)
    mixed_out, grad_query, grad_key, grad_value, cols = grouped_conv(
        q2, k2, v2, g2, prev_tail, next_head, fp, fq, mask, mask_t)
    local_raw = cols.reshape(-1, 2 * FLEN)[:, 2 * FLEN - 1:FLEN - 1:-1]
    summed = doubling_sum(doubling_sum(local_raw, "dp", mirror_masks(lax.axis_size("dp"))), "ctx", ctx_masks())
    squares = doubling_sum(jnp.sum(summed * summed), "tensor", mirror_masks(lax.axis_size("tensor")))
    factor = jnp.minimum(1.0, math.sqrt(GROUPS * FLEN) / jnp.sqrt(squares))
    grad_filters = summed * factor
    return (mixed_out[None], grad_query[None], grad_key[None], grad_value[None], grad_filters)


def solution(mesh):
    tok = P("dp", "ctx", "tensor")
    in_specs = (tok, tok, tok, tok, P("dp", None), P("tensor", None))
    out_specs = (tok, tok, tok, tok, P("tensor", None))
    return jax.shard_map(
        on_device, mesh=mesh, in_specs=in_specs, out_specs=out_specs, check_vma=False
    )
```

```python
import math

import jax
import jax.numpy as jnp
from jax import lax
from jax.experimental import pallas as pl
from jax.experimental.pallas import tpu as pltpu
from jax.sharding import PartitionSpec as P

GROUP = 16
FLEN = 128
GROUPS = 512
LANES = 128


def passed_along(value, axis, steps):
    count = lax.axis_size(axis)
    initial, last = (max(0, -steps), min(count, count - steps))
    return lax.ppermute(value, axis, [(source, source + steps) for source in range(initial, last)])


def doubling_sum(value, axis, masks):
    count = lax.axis_size(axis)
    for mask in masks:
        partner = lax.ppermute(value, axis, [(i, i ^ mask) for i in range(count)])
        value = value + partner
    return value


def conv_kernel(q_ref, k_ref, v_ref, go_ref, prev_ref, next_ref, fp_ref, fq_ref, m_ref, mt_ref, mr_ref,
                mo_ref, gq_ref, gk_ref, gv_ref, raw_ref):
    f32, bf16 = jnp.float32, jnp.bfloat16
    rows = q_ref.shape[0]
    blocks = rows // FLEN
    query = q_ref[...].astype(f32)
    keys = k_ref[...].astype(f32)
    values = v_ref[...].astype(f32)
    upstream = go_ref[...].astype(f32)
    gated = (keys * values).astype(bf16)
    cot = (upstream * query).astype(bf16)
    u_all = jnp.concatenate([prev_ref[...], gated], axis=0)
    c_all = jnp.concatenate([cot, next_ref[...]], axis=0)
    lane_group = lax.broadcasted_iota(jnp.int32, (1, LANES), 1) // GROUP
    windows = [u_all[b * FLEN:(b + 2) * FLEN] for b in range(blocks)]
    cots = [c_all[b * FLEN:(b + 1) * FLEN] for b in range(blocks + 1)]
    masks = [m_ref[b] for b in range(blocks + 1)]
    masks_t = [mt_ref[b] for b in range(blocks + 1)]
    masks_r = [mr_ref[b].astype(f32) for b in range(blocks)]
    flip = (lax.broadcasted_iota(jnp.int32, (FLEN, FLEN), 0)
            + lax.broadcasted_iota(jnp.int32, (FLEN, FLEN), 1) == FLEN - 1).astype(bf16)
    cots_r = [jnp.dot(flip, cots[b], preferred_element_type=f32).astype(bf16) for b in range(blocks)]
    cots_t = [c.astype(f32).T.astype(bf16) for c in cots]
    windows_t = [w.astype(f32).T.astype(bf16) for w in windows]
    mixed_t = [[] for _ in range(blocks)]
    own_t = [[] for _ in range(blocks)]
    spill_t = [[] for _ in range(blocks)]
    nt = (((1,), (1,)), ((), ()))
    sums = []
    for k in range(LANES // GROUP):
        prow = jnp.broadcast_to(fp_ref[k:k + 1, :], (FLEN, 2 * FLEN))
        taps = pltpu.roll(prow, 0, 1, stride=1, stride_axis=0).astype(bf16)
        rows_k = slice(k * GROUP, (k + 1) * GROUP)
        in_group = lane_group == k
        acc = jnp.zeros((FLEN, 2 * FLEN), f32)
        for b in range(blocks + 1):
            group_cot_t = cots_t[b][rows_k]
            if b < blocks:
                operator = taps * masks[b]
                mixed_t[b].append(lax.dot_general(windows_t[b][rows_k], operator, nt, preferred_element_type=f32))
                own_t[b].append(jnp.dot(group_cot_t, operator[:, FLEN:], preferred_element_type=f32))
                group_cot = jnp.where(in_group, cots_r[b], jnp.zeros_like(cots_r[b]))
                prods = lax.dot_general(group_cot, windows[b], nt, preferred_element_type=f32)
                acc = acc + prods * masks_r[b]
            if b > 0:
                lead = taps[:, :FLEN] * masks[b][:, :FLEN]
                spill_t[b - 1].append(jnp.dot(group_cot_t, lead, preferred_element_type=f32))
        skewed = pltpu.roll(acc, 0, 1, stride=1, stride_axis=0)
        sums.append(jnp.sum(skewed, axis=0, keepdims=True))
    raw_ref[0] = jnp.concatenate(sums, axis=0)
    mixed_all = jnp.concatenate([jnp.concatenate(m, axis=0).T for m in mixed_t], axis=0)
    back_all = jnp.concatenate(
        [(jnp.concatenate(own_t[b], axis=0) + jnp.concatenate(spill_t[b], axis=0)).T for b in range(blocks)], axis=0)
    mo_ref[...] = (query * mixed_all).astype(bf16)
    gq_ref[...] = (upstream * mixed_all).astype(bf16)
    gk_ref[...] = (back_all * values).astype(bf16)
    gv_ref[...] = (back_all * keys).astype(bf16)


def grouped_conv(q2, k2, v2, g2, prev_tail, next_head, fp, fq, mask, mask_t, interpret=False):
    mask_r = mask[:-1, ::-1, :]
    rows, channels = q2.shape
    tiles = channels // LANES
    per_tile = LANES // GROUP
    nb = rows // FLEN
    tok = pl.BlockSpec((rows, LANES), lambda j: (0, j))
    halo = pl.BlockSpec((FLEN, LANES), lambda j: (0, j))
    filt = pl.BlockSpec((per_tile, 2 * FLEN), lambda j: (j, 0))
    mspec = pl.BlockSpec((nb + 1, FLEN, 2 * FLEN), lambda j: (0, 0, 0))
    mtspec = pl.BlockSpec((nb + 1, 2 * FLEN, FLEN), lambda j: (0, 0, 0))
    mrspec = pl.BlockSpec((nb, FLEN, 2 * FLEN), lambda j: (0, 0, 0))
    out_tok = jax.ShapeDtypeStruct((rows, channels), jnp.bfloat16)
    return pl.pallas_call(
        conv_kernel,
        grid=(tiles,),
        in_specs=[tok, tok, tok, tok, halo, halo, filt, filt, mspec, mtspec, mrspec],
        out_specs=[tok, tok, tok, tok, pl.BlockSpec((1, per_tile, 2 * FLEN), lambda j: (j, 0, 0))],
        out_shape=[out_tok, out_tok, out_tok, out_tok,
                   jax.ShapeDtypeStruct((tiles, per_tile, 2 * FLEN), jnp.float32)],
        interpret=interpret,
    )(q2, k2, v2, g2, prev_tail, next_head, fp, fq, mask, mask_t, mask_r)


def doc_masks(lengths, offset, rows):
    starts = jnp.cumsum(lengths) - lengths
    nb = rows // FLEN
    b_ids = jnp.arange(nb + 1, dtype=jnp.int32)[:, None]
    tpos = offset + b_ids * FLEN + jnp.arange(FLEN, dtype=jnp.int32)[None, :]
    doc_begin = jnp.max(jnp.where(starts[None, None, :] <= tpos[:, :, None], starts[None, None, :], 0), axis=2)
    rpos = offset + (b_ids - 1) * FLEN + jnp.arange(2 * FLEN, dtype=jnp.int32)[None, :]
    lag = jnp.arange(FLEN, dtype=jnp.int32)[:, None] + FLEN - jnp.arange(2 * FLEN, dtype=jnp.int32)[None, :]
    inside = (lag >= 0) & (lag < FLEN)
    mask = ((rpos[:, None, :] >= doc_begin[:, :, None]) & inside[None]).astype(jnp.bfloat16)
    return mask, mask.transpose(0, 2, 1)


def filter_rows(filters):
    taps = filters.astype(jnp.float32)
    groups = taps.shape[0]
    fp = jnp.concatenate([jnp.zeros((groups, 1), jnp.float32), taps[:, ::-1],
                          jnp.zeros((groups, FLEN - 1), jnp.float32)], axis=1)
    fq = jnp.concatenate([taps, jnp.zeros((groups, FLEN), jnp.float32)], axis=1)
    return fp, fq


def mirror_masks(count):
    masks, width = [], 1
    while width < count:
        masks.append(2 * width - 1)
        width *= 2
    return masks


def ctx_masks():
    inner = 8 if lax.axis_size("ctx") % 8 == 0 else 1
    outer = lax.axis_size("ctx") // inner
    low = [1, 2, 6][: inner.bit_length() - 1]
    return [m * inner for m in mirror_masks(outer)] + low


def on_device(query_in, key_in, value_in, grad_out, seq_lengths, filters):
    f32, bf16 = jnp.float32, jnp.bfloat16
    q2, k2, v2, g2 = query_in[0], key_in[0], value_in[0], grad_out[0]
    rows = q2.shape[0]
    tail = (k2[rows - FLEN:].astype(f32) * v2[rows - FLEN:].astype(f32)).astype(bf16)
    head = (g2[:FLEN].astype(f32) * q2[:FLEN].astype(f32)).astype(bf16)
    prev_tail = passed_along(tail, "ctx", 1)
    next_head = passed_along(head, "ctx", -1)
    mask, mask_t = doc_masks(seq_lengths[0], lax.axis_index("ctx") * rows, rows)
    fp, fq = filter_rows(filters)
    mixed_out, grad_query, grad_key, grad_value, cols = grouped_conv(
        q2, k2, v2, g2, prev_tail, next_head, fp, fq, mask, mask_t)
    local_raw = cols.reshape(-1, 2 * FLEN)[:, 2 * FLEN - 1:FLEN - 1:-1]
    summed = doubling_sum(doubling_sum(local_raw, "dp", mirror_masks(lax.axis_size("dp"))), "ctx", ctx_masks())
    squares = doubling_sum(jnp.sum(summed * summed), "tensor", mirror_masks(lax.axis_size("tensor")))
    factor = jnp.minimum(1.0, math.sqrt(GROUPS * FLEN) / jnp.sqrt(squares))
    grad_filters = summed * factor
    return (mixed_out[None], grad_query[None], grad_key[None], grad_value[None], grad_filters)


def solution(mesh):
    tok = P("dp", "ctx", "tensor")
    in_specs = (tok, tok, tok, tok, P("dp", None), P("tensor", None))
    out_specs = (tok, tok, tok, tok, P("tensor", None))
    return jax.shard_map(
        on_device, mesh=mesh, in_specs=in_specs, out_specs=out_specs, check_vma=False
    )
```

```python
import math

import jax
import jax.numpy as jnp
from jax import lax
from jax.experimental import pallas as pl
from jax.experimental.pallas import tpu as pltpu
from jax.sharding import PartitionSpec as P

GROUP = 16
FLEN = 128
GROUPS = 512
LANES = 128


def passed_along(value, axis, steps):
    count = lax.axis_size(axis)
    initial, last = (max(0, -steps), min(count, count - steps))
    return lax.ppermute(value, axis, [(source, source + steps) for source in range(initial, last)])


def doubling_sum(value, axis, masks):
    count = lax.axis_size(axis)
    for mask in masks:
        partner = lax.ppermute(value, axis, [(i, i ^ mask) for i in range(count)])
        value = value + partner
    return value


def conv_kernel(q_ref, k_ref, v_ref, go_ref, prev_ref, next_ref, fp_ref, fq_ref, m_ref, mt_ref, mr_ref,
                mo_ref, gq_ref, gk_ref, gv_ref, raw_ref):
    f32, bf16 = jnp.float32, jnp.bfloat16
    rows = q_ref.shape[0]
    blocks = rows // FLEN
    query = q_ref[...].astype(f32)
    keys = k_ref[...].astype(f32)
    values = v_ref[...].astype(f32)
    upstream = go_ref[...].astype(f32)
    gated = (keys * values).astype(bf16)
    cot = (upstream * query).astype(bf16)
    u_all = jnp.concatenate([prev_ref[...], gated], axis=0)
    c_all = jnp.concatenate([cot, next_ref[...]], axis=0)
    lane_group = lax.broadcasted_iota(jnp.int32, (1, LANES), 1) // GROUP
    windows = [u_all[b * FLEN:(b + 2) * FLEN] for b in range(blocks)]
    cots = [c_all[b * FLEN:(b + 1) * FLEN] for b in range(blocks + 1)]
    masks = [m_ref[b] for b in range(blocks + 1)]
    masks_t = [mt_ref[b] for b in range(blocks + 1)]
    masks_r = [mr_ref[b].astype(f32) for b in range(blocks)]
    flip = (lax.broadcasted_iota(jnp.int32, (FLEN, FLEN), 0)
            + lax.broadcasted_iota(jnp.int32, (FLEN, FLEN), 1) == FLEN - 1).astype(bf16)
    cots_r = [jnp.dot(flip, cots[b], preferred_element_type=f32).astype(bf16) for b in range(blocks)]
    cots_t = [c.astype(f32).T.astype(bf16) for c in cots]
    windows_t = [w.astype(f32).T.astype(bf16) for w in windows]
    mixed_t = [[] for _ in range(blocks)]
    own_t = [[] for _ in range(blocks)]
    spill_t = [[] for _ in range(blocks)]
    nt = (((1,), (1,)), ((), ()))
    sums = []
    for k in range(LANES // GROUP):
        prow = jnp.broadcast_to(fp_ref[k:k + 1, :], (FLEN, 2 * FLEN))
        taps = pltpu.roll(prow, 0, 1, stride=1, stride_axis=0).astype(bf16)
        rows_k = slice(k * GROUP, (k + 1) * GROUP)
        in_group = lane_group == k
        acc = jnp.zeros((FLEN, 2 * FLEN), f32)
        for b in range(blocks + 1):
            group_cot_t = cots_t[b][rows_k]
            if b < blocks:
                operator = taps * masks[b]
                mixed_t[b].append(lax.dot_general(windows_t[b][rows_k], operator, nt, preferred_element_type=f32))
                own_t[b].append(jnp.dot(group_cot_t, operator[:, FLEN:], preferred_element_type=f32))
                group_cot = jnp.where(in_group, cots_r[b], jnp.zeros_like(cots_r[b]))
                prods = lax.dot_general(group_cot, windows[b], nt, preferred_element_type=f32)
                acc = acc + prods * masks_r[b]
            if b > 0:
                lead = taps[:, :FLEN] * masks[b][:, :FLEN]
                spill_t[b - 1].append(jnp.dot(group_cot_t, lead, preferred_element_type=f32))
        skewed = pltpu.roll(acc, 0, 1, stride=1, stride_axis=0)
        sums.append(jnp.sum(skewed, axis=0, keepdims=True))
    raw_ref[0] = jnp.concatenate(sums, axis=0)
    mixed_all = jnp.concatenate([jnp.concatenate(m, axis=0).T for m in mixed_t], axis=0)
    back_all = jnp.concatenate(
        [(jnp.concatenate(own_t[b], axis=0) + jnp.concatenate(spill_t[b], axis=0)).T for b in range(blocks)], axis=0)
    mo_ref[...] = (query * mixed_all).astype(bf16)
    gq_ref[...] = (upstream * mixed_all).astype(bf16)
    gk_ref[...] = (back_all * values).astype(bf16)
    gv_ref[...] = (back_all * keys).astype(bf16)


def grouped_conv(q2, k2, v2, g2, prev_tail, next_head, fp, fq, mask, mask_t, interpret=False):
    mask_r = mask[:-1, ::-1, :]
    rows, channels = q2.shape
    tiles = channels // LANES
    per_tile = LANES // GROUP
    nb = rows // FLEN
    tok = pl.BlockSpec((rows, LANES), lambda j: (0, j))
    halo = pl.BlockSpec((FLEN, LANES), lambda j: (0, j))
    filt = pl.BlockSpec((per_tile, 2 * FLEN), lambda j: (j, 0))
    mspec = pl.BlockSpec((nb + 1, FLEN, 2 * FLEN), lambda j: (0, 0, 0))
    mtspec = pl.BlockSpec((nb + 1, 2 * FLEN, FLEN), lambda j: (0, 0, 0))
    mrspec = pl.BlockSpec((nb, FLEN, 2 * FLEN), lambda j: (0, 0, 0))
    out_tok = jax.ShapeDtypeStruct((rows, channels), jnp.bfloat16)
    return pl.pallas_call(
        conv_kernel,
        grid=(tiles,),
        in_specs=[tok, tok, tok, tok, halo, halo, filt, filt, mspec, mtspec, mrspec],
        out_specs=[tok, tok, tok, tok, pl.BlockSpec((1, per_tile, 2 * FLEN), lambda j: (j, 0, 0))],
        out_shape=[out_tok, out_tok, out_tok, out_tok,
                   jax.ShapeDtypeStruct((tiles, per_tile, 2 * FLEN), jnp.float32)],
        interpret=interpret,
    )(q2, k2, v2, g2, prev_tail, next_head, fp, fq, mask, mask_t, mask_r)


def doc_masks(lengths, offset, rows):
    starts = jnp.cumsum(lengths) - lengths
    nb = rows // FLEN
    b_ids = jnp.arange(nb + 1, dtype=jnp.int32)[:, None]
    tpos = offset + b_ids * FLEN + jnp.arange(FLEN, dtype=jnp.int32)[None, :]
    doc_begin = jnp.max(jnp.where(starts[None, None, :] <= tpos[:, :, None], starts[None, None, :], 0), axis=2)
    rpos = offset + (b_ids - 1) * FLEN + jnp.arange(2 * FLEN, dtype=jnp.int32)[None, :]
    lag = jnp.arange(FLEN, dtype=jnp.int32)[:, None] + FLEN - jnp.arange(2 * FLEN, dtype=jnp.int32)[None, :]
    inside = (lag >= 0) & (lag < FLEN)
    mask = ((rpos[:, None, :] >= doc_begin[:, :, None]) & inside[None]).astype(jnp.bfloat16)
    return mask, mask.transpose(0, 2, 1)


def filter_rows(filters):
    taps = filters.astype(jnp.float32)
    groups = taps.shape[0]
    fp = jnp.concatenate([jnp.zeros((groups, 1), jnp.float32), taps[:, ::-1],
                          jnp.zeros((groups, FLEN - 1), jnp.float32)], axis=1)
    fq = jnp.concatenate([taps, jnp.zeros((groups, FLEN), jnp.float32)], axis=1)
    return fp, fq


def mirror_masks(count):
    masks, width = [], 1
    while width < count:
        masks.append(2 * width - 1)
        width *= 2
    return masks


def ctx_masks():
    inner = 8 if lax.axis_size("ctx") % 8 == 0 else 1
    outer = lax.axis_size("ctx") // inner
    low = [1, 2, 6][: inner.bit_length() - 1]
    return [m * inner for m in mirror_masks(outer)] + low


def on_device(query_in, key_in, value_in, grad_out, seq_lengths, filters):
    f32, bf16 = jnp.float32, jnp.bfloat16
    q2, k2, v2, g2 = query_in[0], key_in[0], value_in[0], grad_out[0]
    rows = q2.shape[0]
    tail = (k2[rows - FLEN:].astype(f32) * v2[rows - FLEN:].astype(f32)).astype(bf16)
    head = (g2[:FLEN].astype(f32) * q2[:FLEN].astype(f32)).astype(bf16)
    tail, head = lax.optimization_barrier((tail, head))
    prev_tail = passed_along(tail, "ctx", 1)
    next_head = passed_along(head, "ctx", -1)
    mask, mask_t = doc_masks(seq_lengths[0], lax.axis_index("ctx") * rows, rows)
    fp, fq = filter_rows(filters)
    mixed_out, grad_query, grad_key, grad_value, cols = grouped_conv(
        q2, k2, v2, g2, prev_tail, next_head, fp, fq, mask, mask_t)
    local_raw = cols.reshape(-1, 2 * FLEN)[:, 2 * FLEN - 1:FLEN - 1:-1]
    summed = doubling_sum(doubling_sum(local_raw, "dp", mirror_masks(lax.axis_size("dp"))), "ctx", ctx_masks())
    squares = doubling_sum(jnp.sum(summed * summed), "tensor", mirror_masks(lax.axis_size("tensor")))
    factor = jnp.minimum(1.0, math.sqrt(GROUPS * FLEN) / jnp.sqrt(squares))
    grad_filters = summed * factor
    return (mixed_out[None], grad_query[None], grad_key[None], grad_value[None], grad_filters)


def solution(mesh):
    tok = P("dp", "ctx", "tensor")
    in_specs = (tok, tok, tok, tok, P("dp", None), P("tensor", None))
    out_specs = (tok, tok, tok, tok, P("tensor", None))
    return jax.shard_map(
        on_device, mesh=mesh, in_specs=in_specs, out_specs=out_specs, check_vma=False
    )
```
